32 devices in a mesh: vx: 2 (over x), vy: 4 (over z), col: 4 (over y, core).
Axes of the slice: x: 2, y: 2, z: 4, core: 2. Of those that a mesh axis runs over, the one named last changes fastest.
Arguments:
- right_side: float32 [128, 8192], P('col', ('vx', 'vy')), may hold values from -40 to 40
- shift: float32 [8192], P(('vx', 'vy')), may hold values from 0.5 to 5
- edge_ends: int32 [2, 131072], P(None, ('vx', 'vy')), may hold values from 0 to 1535, as said below
- weights: float32 [131072], P(('vx', 'vy')), may hold values from 0.2 to 2
- halo_rows: int32 [64, 64], P(('vx', 'vy')), may hold values from 0 to 1023, as said below
Outputs:
- solution: float32 [128, 8192], P('col', ('vx', 'vy'))
- resistance: float32 [131072], P(('vx', 'vy'))
The draws below stay inside these ranges and needn't reach their ends.
Inputs may be any that keep to these rules, and one draw needn't show every extreme that they name: edge_ends[0] holds local rows below 1024; edge_ends[1] holds a local row below 1024 or 1024 plus a mirror slot; every one of a partition's 8 * 64 mirror slots is named by some edge of it. `halo_rows`: each row lists 64 distinct local rows.
All inputs are finite; a program needn't handle non-finite values.
Results may differ from the reference program's by a relative error of at most 0.0001.
Values sent between devices are 32-bit elements; how exact they have to be, the bound alone decides.
No kernel may reach another device: no remote copies, remote signals or barrier semaphores. Data moves between devices by JAX's collectives and lax.ppermute only.
A program may use at most 64 MiB of HBM per device.

```python
import math
import jax
import jax.numpy as jnp
from jax import lax

COLS = 128
VD = 1024
EDGE_DEV = 16384
CAP = 64
ITERS = 2
NPART = 8
VERT = 8192
EDGES = 131072


def draw_right_side(key, part):
    key_values, key_scale = jax.random.split(jax.random.fold_in(key, 7))
    values = jnp.clip(jax.random.normal(key_values, (COLS, VERT), jnp.float32), -4.0, 4.0)
    scales = jnp.exp(jax.random.uniform(key_scale, (COLS, 1), jnp.float32, math.log(0.3), math.log(3.0)))
    ramp = 1.0 + 2.0 * jnp.arange(VERT, dtype=jnp.float32)[None, :] / VERT
    return (values * scales * ramp).astype(jnp.float32)


def draw_edge_ends(key, part):
    key_head, key_tail, key_cover = jax.random.split(jax.random.fold_in(key, 11), 3)
    base = jax.random.randint(key_head, (NPART, EDGE_DEV), 0, VD)
    head_rows = base * base // VD
    tail_slots = jax.random.randint(key_tail, (NPART, EDGE_DEV), 0, VD + NPART * CAP)
    cover_keys = jax.random.split(key_cover, NPART)
    cover = jax.vmap(lambda item: jax.random.permutation(item, NPART * CAP))(cover_keys) + VD
    tail_slots = tail_slots.at[:, :NPART * CAP].set(cover)
    return jnp.stack([head_rows.reshape(-1), tail_slots.reshape(-1)]).astype(jnp.int32)


def draw_halo_rows(key, part):
    row_keys = jax.random.split(jax.random.fold_in(key, 13), NPART * NPART)
    chosen = jax.vmap(lambda item: jax.random.permutation(item, VD)[:CAP])(row_keys)
    return chosen.astype(jnp.int32)


def level_of(key, shape, pieces, least, largest):
    factor_of, own = 1.0, jax.random.fold_in(key, 6)
    for axis_at, shards_of in pieces:
        steps = jnp.exp(jax.random.uniform(jax.random.fold_in(own, axis_at), (shards_of,), jnp.float32, least / len(pieces), largest / len(pieces)))
        factor_of = factor_of * jnp.repeat(steps, shape[axis_at] // shards_of).reshape([-1 if axis == axis_at else 1 for axis in range(len(shape))])
    return factor_of


def setup_inputs(seed: int = 0) -> dict:
    keys = jax.random.split(jax.random.key(seed), 6)
    right_side = draw_right_side(jax.random.fold_in(keys[5], 71), 0)
    shift = jnp.clip(jnp.exp(math.log(5.0) - 2.3025851 * jax.random.uniform(keys[1], (VERT,), jnp.float32) ** level_of(keys[1], (VERT,), ((0, 8),), -0.2, 0.2)), 0.5, 5.0)
    edge_ends = draw_edge_ends(jax.random.fold_in(keys[5], 71), 0)
    weights = jnp.clip(jnp.exp(math.log(2.0) - 2.3025851 * jax.random.uniform(keys[3], (EDGES,), jnp.float32) ** level_of(keys[3], (EDGES,), ((0, 8),), -0.2, 0.2)), 0.2, 2.0)
    halo_rows = draw_halo_rows(jax.random.fold_in(keys[5], 71), 0)
    return dict(right_side=right_side, shift=shift, edge_ends=edge_ends, weights=weights, halo_rows=halo_rows)


def endpoints(edge_ends, halo_rows):
    part = jnp.arange(NPART, dtype=jnp.int32)[:, None]
    head_rows = edge_ends[0].reshape(NPART, EDGE_DEV)
    tail_slots = edge_ends[1].reshape(NPART, EDGE_DEV)
    slot = jnp.clip(tail_slots - VD, 0, NPART * CAP - 1)
    peer = slot // CAP
    within = slot % CAP
    table = halo_rows.reshape(NPART, NPART, CAP)
    remote = table[peer, jnp.broadcast_to(part, peer.shape), within]
    head = (part * VD + head_rows).reshape(-1).astype(jnp.int32)
    tail = jnp.where(tail_slots < VD, part * VD + tail_slots, peer * VD + remote).reshape(-1).astype(jnp.int32)
    return head, tail


def operate(field, shift, head, tail, weights):
    groups = field.reshape(COLS // 8, 8, VERT)

    def one_group(block):
        flow = (block[:, head] - block[:, tail]) * weights
        summed = jnp.zeros(block.shape, jnp.float32).at[:, head].add(flow).at[:, tail].add(-flow)
        return shift * block + summed

    return lax.map(one_group, groups).reshape(COLS, VERT)


def reference(right_side, shift, edge_ends, weights, halo_rows):
    head, tail = endpoints(edge_ends, halo_rows)
    solution = jnp.zeros_like(right_side)
    residual = right_side
    direction = right_side
    norm_now = jnp.sum(residual * residual, axis=1)
    for step in range(ITERS):
        image = operate(direction, shift, head, tail, weights)
        alpha = norm_now / jnp.sum(direction * image, axis=1)
        solution = solution + alpha[:, None] * direction
        residual = residual - alpha[:, None] * image
        norm_next = jnp.sum(residual * residual, axis=1)
        direction = residual + (norm_next / norm_now)[:, None] * direction
        norm_now = norm_next
    groups = solution.reshape(COLS // 8, 8, VERT)

    def squared(block):
        gap = block[:, head] - block[:, tail]
        return jnp.sum(gap * gap, axis=0)

    resistance = jnp.sum(lax.map(squared, groups), axis=0)
    return solution, resistance
```

```python
import jax
import jax.numpy as jnp
from jax import lax
from jax.experimental import pallas as pl
from jax.experimental.pallas import tpu as pltpu
from jax.sharding import PartitionSpec as P

ITERS = 2


def trade(blocks):
    return lax.all_to_all(blocks, ("vx", "vy"), split_axis=1, concat_axis=1, tiled=True)


def split3(values):
    first = values.astype(jnp.bfloat16)
    rest = values - first.astype(jnp.float32)
    second = rest.astype(jnp.bfloat16)
    third = (rest - second.astype(jnp.float32)).astype(jnp.bfloat16)
    return jnp.concatenate([first, second, third], axis=0)


def edge_tile(rows):
    return 1024 if rows <= 2048 else 256


def flow_kernel(local, scatter):
    def kernel(xs_ref, head_ref, tail_ref, w_ref, out_ref, *acc):
        step = pl.program_id(0)
        width, rows = xs_ref.shape
        tile = head_ref.shape[1]
        head = head_ref[...]
        tail = tail_ref[...]
        g_head = (lax.broadcasted_iota(jnp.int32, (local, tile), 0) == head).astype(jnp.bfloat16)
        g_tail = (lax.broadcasted_iota(jnp.int32, (rows, tile), 0) == tail).astype(jnp.bfloat16)
        xs = split3(xs_ref[...])
        near = jnp.dot(xs[:, :local], g_head, preferred_element_type=jnp.float32)
        far = jnp.dot(xs, g_tail, preferred_element_type=jnp.float32)
        gap = near - far
        gap = gap[:width] + gap[width:2 * width] + gap[2 * width:]
        if not scatter:
            out_ref[...] = jnp.sum(gap * gap, axis=0, keepdims=True)
            return
        acc_head, acc_tail = acc

        flow = split3(gap * w_ref[...])
        dims = (((1,), (1,)), ((), ()))
        first = step == 0
        acc_head[...] = jnp.where(first, 0.0, acc_head[...]) + lax.dot_general(
            flow, g_head, dims, preferred_element_type=jnp.float32
        )
        acc_tail[...] = jnp.where(first, 0.0, acc_tail[...]) + lax.dot_general(
            flow, g_tail, dims, preferred_element_type=jnp.float32
        )

        @pl.when(step == pl.num_programs(0) - 1)
        def _():
            th = acc_head[...]
            tt = acc_tail[...]
            th = th[:width] + th[width:2 * width] + th[2 * width:]
            tt = tt[:width] + tt[width:2 * width] + tt[2 * width:]
            out_ref[:, :local] = th - tt[:, :local]
            out_ref[:, local:] = -tt[:, local:]

    return kernel


def edge_pass(extended, head_rows, tail_slots, weights, local, scatter):
    width, rows = extended.shape
    edges = head_rows.shape[1]
    tile = edge_tile(rows)
    edge_spec = pl.BlockSpec((1, tile), lambda i: (0, i))
    full = pl.BlockSpec((width, rows), lambda i: (0, 0))
    if scatter:
        out_shape = jax.ShapeDtypeStruct((width, rows), jnp.float32)
        out_spec = pl.BlockSpec((width, rows), lambda i: (0, 0))
        scratch = [pltpu.VMEM((3 * width, local), jnp.float32), pltpu.VMEM((3 * width, rows), jnp.float32)]
    else:
        out_shape = jax.ShapeDtypeStruct((1, edges), jnp.float32)
        out_spec = edge_spec
        scratch = []
    return pl.pallas_call(
        flow_kernel(local, scatter),
        grid=(edges // tile,),
        in_specs=[full, edge_spec, edge_spec, edge_spec],
        out_specs=out_spec,
        out_shape=out_shape,
        scratch_shapes=scratch,
        compiler_params=pltpu.CompilerParams(
            dimension_semantics=("arbitrary",), vmem_limit_bytes=48 * 1024 * 1024
        ),
    )(extended, head_rows, tail_slots, weights)


def extend(field, halo_rows):
    mirrored = trade(field[:, halo_rows])
    return jnp.concatenate([field, mirrored.reshape(field.shape[0], -1)], axis=1)


def operate(field, shift, head_rows, tail_slots, weights, halo_rows):
    count = field.shape[1]
    width = field.shape[0]
    extended = extend(field, halo_rows)
    summed = edge_pass(extended, head_rows, tail_slots, weights, count, True)
    returned = trade(summed[:, count:].reshape(width, halo_rows.shape[0], halo_rows.shape[1]))
    local = summed[:, :count].at[:, halo_rows.reshape(-1)].add(returned.reshape(width, -1))
    return shift * field + local


def two_products(residual, image):
    return lax.psum(
        (jnp.sum(residual * residual, axis=1), jnp.sum(residual * image, axis=1)), ("vx", "vy")
    )


def body(right_side, shift, edge_ends, weights, halo_rows):
    head_rows = edge_ends[0:1]
    tail_slots = edge_ends[1:2]
    weights = weights[None, :]
    solution = jnp.zeros_like(right_side)
    residual = right_side
    image = operate(residual, shift, head_rows, tail_slots, weights, halo_rows)
    norm_now, product = two_products(residual, image)
    alpha = norm_now / product
    direction = residual
    along = image
    for step in range(ITERS):
        solution = solution + alpha[:, None] * direction
        residual = residual - alpha[:, None] * along
        if step + 1 < ITERS:
            image = operate(residual, shift, head_rows, tail_slots, weights, halo_rows)
            norm_next, product = two_products(residual, image)
            ratio = norm_next / norm_now
            alpha = norm_next / (product - ratio * norm_next / alpha)
            direction = residual + ratio[:, None] * direction
            along = image + ratio[:, None] * along
            norm_now = norm_next
    extended = extend(solution, halo_rows)
    partial_total = edge_pass(extended, head_rows, tail_slots, weights, solution.shape[1], False)[0]
    resistance = lax.psum(partial_total, "col")
    return (solution, resistance)


def solution(mesh):
    placed = (
        P("col", ("vx", "vy")),
        P(("vx", "vy")),
        P(None, ("vx", "vy")),
        P(("vx", "vy")),
        P(("vx", "vy"), None),
    )
    return jax.shard_map(
        body,
        mesh=mesh,
        in_specs=placed,
        out_specs=(P("col", ("vx", "vy")), P(("vx", "vy"))),
        check_vma=False,
    )
```

```python
import jax
import jax.numpy as jnp
from jax import lax
from jax.experimental import pallas as pl
from jax.experimental.pallas import tpu as pltpu
from jax.sharding import PartitionSpec as P

ITERS = 2


def trade(blocks):
    return lax.all_to_all(blocks, ("vx", "vy"), split_axis=1, concat_axis=1, tiled=True)


def split3(values):
    first = values.astype(jnp.bfloat16)
    rest = values - first.astype(jnp.float32)
    second = rest.astype(jnp.bfloat16)
    third = (rest - second.astype(jnp.float32)).astype(jnp.bfloat16)
    return jnp.concatenate([first, second, third], axis=0)


def edge_tile(rows):
    return 1024 if rows <= 2048 else 256


def flow_kernel(local, scatter):
    def kernel(xs_ref, head_ref, tail_ref, w_ref, out_ref, *acc):
        step = pl.program_id(0)
        width, rows = xs_ref.shape
        tile = head_ref.shape[1]
        head = head_ref[...]
        tail = tail_ref[...]
        g_head = (lax.broadcasted_iota(jnp.int32, (local, tile), 0) == head).astype(jnp.bfloat16)
        g_tail = (lax.broadcasted_iota(jnp.int32, (rows, tile), 0) == tail).astype(jnp.bfloat16)
        xs = split3(xs_ref[...])
        near = jnp.dot(xs[:, :local], g_head, preferred_element_type=jnp.float32)
        far = jnp.dot(xs, g_tail, preferred_element_type=jnp.float32)
        gap = near - far
        gap = gap[:width] + gap[width:2 * width] + gap[2 * width:]
        if not scatter:
            out_ref[...] = jnp.sum(gap * gap, axis=0, keepdims=True)
            return
        acc_head, acc_tail = acc

        flow = split3(gap * w_ref[...])
        dims = (((1,), (1,)), ((), ()))
        first = step == 0
        acc_head[...] = jnp.where(first, 0.0, acc_head[...]) + lax.dot_general(
            flow, g_head, dims, preferred_element_type=jnp.float32
        )
        acc_tail[...] = jnp.where(first, 0.0, acc_tail[...]) + lax.dot_general(
            flow, g_tail, dims, preferred_element_type=jnp.float32
        )

        @pl.when(step == pl.num_programs(0) - 1)
        def _():
            th = acc_head[...]
            tt = acc_tail[...]
            th = th[:width] + th[width:2 * width] + th[2 * width:]
            tt = tt[:width] + tt[width:2 * width] + tt[2 * width:]
            out_ref[:, :local] = th - tt[:, :local]
            out_ref[:, local:] = -tt[:, local:]

    return kernel


def edge_pass(extended, head_rows, tail_slots, weights, local, scatter):
    width, rows = extended.shape
    edges = head_rows.shape[1]
    tile = edge_tile(rows)
    edge_spec = pl.BlockSpec((1, tile), lambda i: (0, i))
    full = pl.BlockSpec((width, rows), lambda i: (0, 0))
    if scatter:
        out_shape = jax.ShapeDtypeStruct((width, rows), jnp.float32)
        out_spec = pl.BlockSpec((width, rows), lambda i: (0, 0))
        scratch = [pltpu.VMEM((3 * width, local), jnp.float32), pltpu.VMEM((3 * width, rows), jnp.float32)]
    else:
        out_shape = jax.ShapeDtypeStruct((1, edges), jnp.float32)
        out_spec = edge_spec
        scratch = []
    return pl.pallas_call(
        flow_kernel(local, scatter),
        grid=(edges // tile,),
        in_specs=[full, edge_spec, edge_spec, edge_spec],
        out_specs=out_spec,
        out_shape=out_shape,
        scratch_shapes=scratch,
        compiler_params=pltpu.CompilerParams(
            dimension_semantics=("arbitrary",), vmem_limit_bytes=48 * 1024 * 1024
        ),
    )(extended, head_rows, tail_slots, weights)


def extend(field, halo_rows):
    mirrored = trade(field[:, halo_rows])
    return jnp.concatenate([field, mirrored.reshape(field.shape[0], -1)], axis=1)


def gathered(field, halo_rows):
    return lax.all_gather(extend(field, halo_rows), "col", axis=0, tiled=True)


def operate(field, shift, head_rows, tail_slots, weights, halo_rows):
    count = field.shape[1]
    width = field.shape[0]
    partial = edge_pass(gathered(field, halo_rows), head_rows, tail_slots, weights, count, True)
    summed = lax.psum_scatter(partial, "col", scatter_dimension=0, tiled=True)
    returned = trade(summed[:, count:].reshape(width, halo_rows.shape[0], halo_rows.shape[1]))
    local = summed[:, :count].at[:, halo_rows.reshape(-1)].add(returned.reshape(width, -1))
    return shift * field + local


def two_products(residual, image):
    return lax.psum(
        (jnp.sum(residual * residual, axis=1), jnp.sum(residual * image, axis=1)), ("vx", "vy")
    )


def body(right_side, shift, edge_ends, weights, halo_rows):
    groups = lax.axis_size("col")
    share = edge_ends.shape[1] // groups
    start = lax.axis_index("col") * share
    head_rows = lax.dynamic_slice_in_dim(edge_ends[0:1], start, share, axis=1)
    tail_slots = lax.dynamic_slice_in_dim(edge_ends[1:2], start, share, axis=1)
    weights = lax.dynamic_slice_in_dim(weights[None, :], start, share, axis=1)
    solution = jnp.zeros_like(right_side)
    residual = right_side
    image = operate(residual, shift, head_rows, tail_slots, weights, halo_rows)
    norm_now, product = two_products(residual, image)
    alpha = norm_now / product
    direction = residual
    along = image
    for step in range(ITERS):
        solution = solution + alpha[:, None] * direction
        residual = residual - alpha[:, None] * along
        if step + 1 < ITERS:
            image = operate(residual, shift, head_rows, tail_slots, weights, halo_rows)
            norm_next, product = two_products(residual, image)
            ratio = norm_next / norm_now
            alpha = norm_next / (product - ratio * norm_next / alpha)
            direction = residual + ratio[:, None] * direction
            along = image + ratio[:, None] * along
            norm_now = norm_next
    total = edge_pass(gathered(solution, halo_rows), head_rows, tail_slots, weights, solution.shape[1], False)[0]
    resistance = lax.all_gather(total, "col", axis=0, tiled=True)
    return (solution, resistance)


def solution(mesh):
    placed = (
        P("col", ("vx", "vy")),
        P(("vx", "vy")),
        P(None, ("vx", "vy")),
        P(("vx", "vy")),
        P(("vx", "vy"), None),
    )
    return jax.shard_map(
        body,
        mesh=mesh,
        in_specs=placed,
        out_specs=(P("col", ("vx", "vy")), P(("vx", "vy"))),
        check_vma=False,
    )
```

```python
import jax
import jax.numpy as jnp
from jax import lax
from jax.experimental import pallas as pl
from jax.experimental.pallas import tpu as pltpu
from jax.sharding import PartitionSpec as P

ITERS = 2


def trade(blocks):
    return lax.all_to_all(blocks, ("vx", "vy"), split_axis=1, concat_axis=1, tiled=True)


def split3(values):
    first = values.astype(jnp.bfloat16)
    rest = values - first.astype(jnp.float32)
    second = rest.astype(jnp.bfloat16)
    third = (rest - second.astype(jnp.float32)).astype(jnp.bfloat16)
    return jnp.concatenate([first, second, third], axis=0)


def edge_tile(rows):
    return 1024 if rows <= 2048 else 256


def flow_kernel(scatter):
    def kernel(xs_ref, head_ref, tail_ref, w_ref, out_ref, *acc):
        step = pl.program_id(0)
        width, rows = xs_ref.shape
        tile = head_ref.shape[1]
        index = lax.broadcasted_iota(jnp.int32, (rows, tile), 0)
        ends = (index == head_ref[...]).astype(jnp.float32) - (index == tail_ref[...]).astype(jnp.float32)
        ends = ends.astype(jnp.bfloat16)
        gap = jnp.dot(split3(xs_ref[...]), ends, preferred_element_type=jnp.float32)
        gap = gap[:width] + gap[width:2 * width] + gap[2 * width:]
        if not scatter:
            out_ref[...] = jnp.sum(gap * gap, axis=0, keepdims=True)
            return
        (total,) = acc
        flow = split3(gap * w_ref[...])
        dims = (((1,), (1,)), ((), ()))
        total[...] = jnp.where(step == 0, 0.0, total[...]) + lax.dot_general(
            flow, ends, dims, preferred_element_type=jnp.float32
        )

        @pl.when(step == pl.num_programs(0) - 1)
        def _():
            sums = total[...]
            out_ref[...] = sums[:width] + sums[width:2 * width] + sums[2 * width:]

    return kernel


def edge_pass(extended, head_rows, tail_slots, weights, scatter):
    width, rows = extended.shape
    edges = head_rows.shape[1]
    tile = edge_tile(rows)
    edge_spec = pl.BlockSpec((1, tile), lambda i: (0, i))
    full = pl.BlockSpec((width, rows), lambda i: (0, 0))
    if scatter:
        out_shape = jax.ShapeDtypeStruct((width, rows), jnp.float32)
        out_spec = pl.BlockSpec((width, rows), lambda i: (0, 0))
        scratch = [pltpu.VMEM((3 * width, rows), jnp.float32)]
    else:
        out_shape = jax.ShapeDtypeStruct((1, edges), jnp.float32)
        out_spec = edge_spec
        scratch = []
    return pl.pallas_call(
        flow_kernel(scatter),
        grid=(edges // tile,),
        in_specs=[full, edge_spec, edge_spec, edge_spec],
        out_specs=out_spec,
        out_shape=out_shape,
        scratch_shapes=scratch,
        compiler_params=pltpu.CompilerParams(
            dimension_semantics=("arbitrary",), vmem_limit_bytes=48 * 1024 * 1024
        ),
    )(extended, head_rows, tail_slots, weights)


def extend(field, halo_rows):
    mirrored = trade(field[:, halo_rows])
    return jnp.concatenate([field, mirrored.reshape(field.shape[0], -1)], axis=1)


def gathered(field, halo_rows):
    return lax.all_gather(extend(field, halo_rows), "col", axis=0, tiled=True)


def operate(field, shift, head_rows, tail_slots, weights, halo_rows):
    count = field.shape[1]
    width = field.shape[0]
    summed = edge_pass(extend(field, halo_rows), head_rows, tail_slots, weights, True)
    returned = trade(summed[:, count:].reshape(width, halo_rows.shape[0], halo_rows.shape[1]))
    local = summed[:, :count].at[:, halo_rows.reshape(-1)].add(returned.reshape(width, -1))
    return shift * field + local


def two_products(residual, image):
    return lax.psum(
        (jnp.sum(residual * residual, axis=1), jnp.sum(residual * image, axis=1)), ("vx", "vy")
    )


def body(right_side, shift, edge_ends, weights, halo_rows):
    head_rows = edge_ends[0:1]
    tail_slots = edge_ends[1:2]
    weights = weights[None, :]
    share = edge_ends.shape[1] // lax.axis_size("col")
    start = lax.axis_index("col") * share
    quarter = [lax.dynamic_slice_in_dim(item, start, share, axis=1) for item in (head_rows, tail_slots, weights)]
    solution = jnp.zeros_like(right_side)
    residual = right_side
    image = operate(residual, shift, head_rows, tail_slots, weights, halo_rows)
    norm_now, product = two_products(residual, image)
    alpha = norm_now / product
    direction = residual
    along = image
    for step in range(ITERS):
        solution = solution + alpha[:, None] * direction
        residual = residual - alpha[:, None] * along
        if step + 1 < ITERS:
            image = operate(residual, shift, head_rows, tail_slots, weights, halo_rows)
            norm_next, product = two_products(residual, image)
            ratio = norm_next / norm_now
            alpha = norm_next / (product - ratio * norm_next / alpha)
            direction = residual + ratio[:, None] * direction
            along = image + ratio[:, None] * along
            norm_now = norm_next
    total = edge_pass(gathered(solution, halo_rows), *quarter, False)[0]
    resistance = lax.all_gather(total, "col", axis=0, tiled=True)
    return (solution, resistance)


def solution(mesh):
    placed = (
        P("col", ("vx", "vy")),
        P(("vx", "vy")),
        P(None, ("vx", "vy")),
        P(("vx", "vy")),
        P(("vx", "vy"), None),
    )
    return jax.shard_map(
        body,
        mesh=mesh,
        in_specs=placed,
        out_specs=(P("col", ("vx", "vy")), P(("vx", "vy"))),
        check_vma=False,
    )
```

```python
import jax
import jax.numpy as jnp
from jax import lax
from jax.experimental import pallas as pl
from jax.experimental.pallas import tpu as pltpu
from jax.sharding import PartitionSpec as P

ITERS = 2


def trade(blocks):
    return lax.all_to_all(blocks, ("vx", "vy"), split_axis=1, concat_axis=1, tiled=True)


def split3(values):
    first = values.astype(jnp.bfloat16)
    rest = values - first.astype(jnp.float32)
    second = rest.astype(jnp.bfloat16)
    third = (rest - second.astype(jnp.float32)).astype(jnp.bfloat16)
    return jnp.concatenate([first, second, third], axis=0)


def edge_tile(rows):
    return 1024 if rows <= 2048 else 256


def flow_kernel(scatter):
    def kernel(xs_ref, head_ref, tail_ref, w_ref, *out_ref):
        out_ref, acc = (out_ref[:2], out_ref[2:]) if scatter else (out_ref[0], ())
        step = pl.program_id(0)
        width, rows = xs_ref.shape
        tile = head_ref.shape[1]
        index = lax.broadcasted_iota(jnp.int32, (rows, tile), 0)
        ends = (index == head_ref[...]).astype(jnp.float32) - (index == tail_ref[...]).astype(jnp.float32)
        ends = ends.astype(jnp.bfloat16)
        gap = jnp.dot(split3(xs_ref[...]), ends, preferred_element_type=jnp.float32)
        gap = gap[:width] + gap[width:2 * width] + gap[2 * width:]
        if not scatter:
            out_ref[...] = jnp.sum(gap * gap, axis=0, keepdims=True)
            return
        (total,) = acc
        energy_ref = out_ref[1]
        out_ref = out_ref[0]
        weighted = gap * w_ref[...]
        energy = jnp.sum(gap * weighted, axis=1, keepdims=True)
        energy_ref[...] = jnp.where(step == 0, 0.0, energy_ref[...]) + energy
        flow = split3(weighted)
        dims = (((1,), (1,)), ((), ()))
        total[...] = jnp.where(step == 0, 0.0, total[...]) + lax.dot_general(
            flow, ends, dims, preferred_element_type=jnp.float32
        )

        @pl.when(step == pl.num_programs(0) - 1)
        def _():
            sums = total[...]
            out_ref[...] = sums[:width] + sums[width:2 * width] + sums[2 * width:]

    return kernel


def edge_pass(extended, head_rows, tail_slots, weights, scatter):
    width, rows = extended.shape
    edges = head_rows.shape[1]
    tile = edge_tile(rows)
    edge_spec = pl.BlockSpec((1, tile), lambda i: (0, i))
    full = pl.BlockSpec((width, rows), lambda i: (0, 0))
    if scatter:
        out_shape = (jax.ShapeDtypeStruct((width, rows), jnp.float32), jax.ShapeDtypeStruct((width, 1), jnp.float32))
        out_spec = (pl.BlockSpec((width, rows), lambda i: (0, 0)), pl.BlockSpec((width, 1), lambda i: (0, 0)))
        scratch = [pltpu.VMEM((3 * width, rows), jnp.float32)]
    else:
        out_shape = jax.ShapeDtypeStruct((1, edges), jnp.float32)
        out_spec = edge_spec
        scratch = []
    return pl.pallas_call(
        flow_kernel(scatter),
        grid=(edges // tile,),
        in_specs=[full, edge_spec, edge_spec, edge_spec],
        out_specs=out_spec,
        out_shape=out_shape,
        scratch_shapes=scratch,
        compiler_params=pltpu.CompilerParams(
            dimension_semantics=("arbitrary",), vmem_limit_bytes=48 * 1024 * 1024
        ),
    )(extended, head_rows, tail_slots, weights)


def extend(field, halo_rows):
    mirrored = trade(field[:, halo_rows])
    return jnp.concatenate([field, mirrored.reshape(field.shape[0], -1)], axis=1)


def gathered(field, halo_rows):
    return lax.all_gather(extend(field, halo_rows), "col", axis=0, tiled=True)


def operate(field, shift, head_rows, tail_slots, weights, halo_rows):
    count = field.shape[1]
    width = field.shape[0]
    peers, cap = halo_rows.shape
    summed, energy = edge_pass(extend(field, halo_rows), head_rows, tail_slots, weights, True)
    squares = field * field
    own = jnp.stack([jnp.sum(squares, axis=1), jnp.sum(shift * squares, axis=1) + energy[:, 0]], axis=1)
    sent = jnp.concatenate(
        [summed[:, count:].reshape(width, peers, cap), jnp.broadcast_to(own[:, None, :], (width, peers, 2))], axis=2
    )
    got = trade(sent)
    returned = got[:, :, :cap].reshape(width, -1)
    norm, product = jnp.sum(got[:, :, cap:], axis=1).T
    local = summed[:, :count].at[:, halo_rows.reshape(-1)].add(returned)
    return shift * field + local, norm, product


def body(right_side, shift, edge_ends, weights, halo_rows):
    head_rows = edge_ends[0:1]
    tail_slots = edge_ends[1:2]
    weights = weights[None, :]
    share = edge_ends.shape[1] // lax.axis_size("col")
    start = lax.axis_index("col") * share
    quarter = [lax.dynamic_slice_in_dim(item, start, share, axis=1) for item in (head_rows, tail_slots, weights)]
    solution = jnp.zeros_like(right_side)
    residual = right_side
    image, norm_now, product = operate(residual, shift, head_rows, tail_slots, weights, halo_rows)
    alpha = norm_now / product
    direction = residual
    along = image
    for step in range(ITERS):
        solution = solution + alpha[:, None] * direction
        residual = residual - alpha[:, None] * along
        if step + 1 < ITERS:
            image, norm_next, product = operate(residual, shift, head_rows, tail_slots, weights, halo_rows)
            ratio = norm_next / norm_now
            alpha = norm_next / (product - ratio * norm_next / alpha)
            direction = residual + ratio[:, None] * direction
            along = image + ratio[:, None] * along
            norm_now = norm_next
    total = edge_pass(gathered(solution, halo_rows), *quarter, False)[0]
    resistance = lax.all_gather(total, "col", axis=0, tiled=True)
    return (solution, resistance)


def solution(mesh):
    placed = (
        P("col", ("vx", "vy")),
        P(("vx", "vy")),
        P(None, ("vx", "vy")),
        P(("vx", "vy")),
        P(("vx", "vy"), None),
    )
    return jax.shard_map(
        body,
        mesh=mesh,
        in_specs=placed,
        out_specs=(P("col", ("vx", "vy")), P(("vx", "vy"))),
        check_vma=False,
    )
```

```python
import jax
import jax.numpy as jnp
from jax import lax
from jax.experimental import pallas as pl
from jax.experimental.pallas import tpu as pltpu
from jax.sharding import PartitionSpec as P

ITERS = 2


def trade(blocks):
    return lax.all_to_all(blocks, ("vx", "vy"), split_axis=1, concat_axis=1, tiled=True)


def split3(values):
    first = values.astype(jnp.bfloat16)
    rest = values - first.astype(jnp.float32)
    second = rest.astype(jnp.bfloat16)
    third = (rest - second.astype(jnp.float32)).astype(jnp.bfloat16)
    return jnp.concatenate([first, second, third], axis=0)


def edge_tile(rows):
    return 2048 if rows <= 2048 else 256


def incidence(head, tail, rows):
    tile = head.shape[1]
    if rows % 128:
        index = lax.broadcasted_iota(jnp.int32, (rows, tile), 0)
        ends = (index == head).astype(jnp.float32) - (index == tail).astype(jnp.float32)
        return ends.astype(jnp.bfloat16)
    lane = lax.broadcasted_iota(jnp.int32, (128, tile), 0)
    low_head = (lane == (head & 127)).astype(jnp.bfloat16)
    low_tail = (lane == (tail & 127)).astype(jnp.bfloat16)
    high_head = head >> 7
    high_tail = tail >> 7
    blocks = []
    for block in range(rows // 128):
        on_head = (high_head == block).astype(jnp.bfloat16)
        on_tail = (high_tail == block).astype(jnp.bfloat16)
        blocks.append(low_head * on_head - low_tail * on_tail)
    return jnp.concatenate(blocks, axis=0)


def flow_kernel(scatter):
    def kernel(xs_ref, head_ref, tail_ref, w_ref, *out_ref):
        out_ref, acc = (out_ref[:2], out_ref[2:]) if scatter else (out_ref[0], ())
        step = pl.program_id(0)
        width, rows = xs_ref.shape
        tile = head_ref.shape[1]
        ends = incidence(head_ref[...], tail_ref[...], rows)
        gap = jnp.dot(split3(xs_ref[...]), ends, preferred_element_type=jnp.float32)
        gap = gap[:width] + gap[width:2 * width] + gap[2 * width:]
        if not scatter:
            out_ref[...] = jnp.sum(gap * gap, axis=0, keepdims=True)
            return
        (total,) = acc
        energy_ref = out_ref[1]
        out_ref = out_ref[0]
        weighted = gap * w_ref[...]
        energy = jnp.sum(gap * weighted, axis=1, keepdims=True)
        energy_ref[...] = jnp.where(step == 0, 0.0, energy_ref[...]) + energy
        flow = split3(weighted)
        dims = (((1,), (1,)), ((), ()))
        total[...] = jnp.where(step == 0, 0.0, total[...]) + lax.dot_general(
            flow, ends, dims, preferred_element_type=jnp.float32
        )

        @pl.when(step == pl.num_programs(0) - 1)
        def _():
            sums = total[...]
            out_ref[...] = sums[:width] + sums[width:2 * width] + sums[2 * width:]

    return kernel


def edge_pass(extended, head_rows, tail_slots, weights, scatter):
    width, rows = extended.shape
    edges = head_rows.shape[1]
    tile = edge_tile(rows)
    edge_spec = pl.BlockSpec((1, tile), lambda i: (0, i))
    full = pl.BlockSpec((width, rows), lambda i: (0, 0))
    if scatter:
        out_shape = (jax.ShapeDtypeStruct((width, rows), jnp.float32), jax.ShapeDtypeStruct((width, 1), jnp.float32))
        out_spec = (pl.BlockSpec((width, rows), lambda i: (0, 0)), pl.BlockSpec((width, 1), lambda i: (0, 0)))
        scratch = [pltpu.VMEM((3 * width, rows), jnp.float32)]
    else:
        out_shape = jax.ShapeDtypeStruct((1, edges), jnp.float32)
        out_spec = edge_spec
        scratch = []
    return pl.pallas_call(
        flow_kernel(scatter),
        grid=(edges // tile,),
        in_specs=[full, edge_spec, edge_spec, edge_spec],
        out_specs=out_spec,
        out_shape=out_shape,
        scratch_shapes=scratch,
        compiler_params=pltpu.CompilerParams(
            dimension_semantics=("arbitrary",), vmem_limit_bytes=48 * 1024 * 1024
        ),
    )(extended, head_rows, tail_slots, weights)


def extend(field, halo_rows):
    mirrored = trade(field[:, halo_rows])
    return jnp.concatenate([field, mirrored.reshape(field.shape[0], -1)], axis=1)


def gathered(field, halo_rows):
    return lax.all_gather(extend(field, halo_rows), "col", axis=0, tiled=True)


def operate(field, shift, head_rows, tail_slots, weights, halo_rows):
    count = field.shape[1]
    width = field.shape[0]
    peers, cap = halo_rows.shape
    summed, energy = edge_pass(extend(field, halo_rows), head_rows, tail_slots, weights, True)
    squares = field * field
    own = jnp.stack([jnp.sum(squares, axis=1), jnp.sum(shift * squares, axis=1) + energy[:, 0]], axis=1)
    sent = jnp.concatenate(
        [summed[:, count:].reshape(width, peers, cap), jnp.broadcast_to(own[:, None, :], (width, peers, 2))], axis=2
    )
    got = trade(sent)
    returned = got[:, :, :cap].reshape(width, -1)
    norm, product = jnp.sum(got[:, :, cap:], axis=1).T
    local = summed[:, :count].at[:, halo_rows.reshape(-1)].add(returned)
    return shift * field + local, norm, product


def body(right_side, shift, edge_ends, weights, halo_rows):
    head_rows = edge_ends[0:1]
    tail_slots = edge_ends[1:2]
    weights = weights[None, :]
    share = edge_ends.shape[1] // lax.axis_size("col")
    start = lax.axis_index("col") * share
    quarter = [lax.dynamic_slice_in_dim(item, start, share, axis=1) for item in (head_rows, tail_slots, weights)]
    solution = jnp.zeros_like(right_side)
    residual = right_side
    image, norm_now, product = operate(residual, shift, head_rows, tail_slots, weights, halo_rows)
    alpha = norm_now / product
    direction = residual
    along = image
    for step in range(ITERS):
        solution = solution + alpha[:, None] * direction
        residual = residual - alpha[:, None] * along
        if step + 1 < ITERS:
            image, norm_next, product = operate(residual, shift, head_rows, tail_slots, weights, halo_rows)
            ratio = norm_next / norm_now
            alpha = norm_next / (product - ratio * norm_next / alpha)
            direction = residual + ratio[:, None] * direction
            along = image + ratio[:, None] * along
            norm_now = norm_next
    total = edge_pass(gathered(solution, halo_rows), *quarter, False)[0]
    resistance = lax.all_gather(total, "col", axis=0, tiled=True)
    return (solution, resistance)


def solution(mesh):
    placed = (
        P("col", ("vx", "vy")),
        P(("vx", "vy")),
        P(None, ("vx", "vy")),
        P(("vx", "vy")),
        P(("vx", "vy"), None),
    )
    return jax.shard_map(
        body,
        mesh=mesh,
        in_specs=placed,
        out_specs=(P("col", ("vx", "vy")), P(("vx", "vy"))),
        check_vma=False,
    )
```

```python
import jax
import jax.numpy as jnp
from jax import lax
from jax.experimental import pallas as pl
from jax.experimental.pallas import tpu as pltpu
from jax.sharding import PartitionSpec as P

ITERS = 2


def trade(blocks):
    return lax.all_to_all(blocks, ("vx", "vy"), split_axis=1, concat_axis=1, tiled=True)


def split3(values):
    first = values.astype(jnp.bfloat16)
    rest = values - first.astype(jnp.float32)
    second = rest.astype(jnp.bfloat16)
    third = (rest - second.astype(jnp.float32)).astype(jnp.bfloat16)
    return jnp.concatenate([first, second, third], axis=0)


def edge_tile(rows):
    return 2048 if rows <= 2048 else 256


def incidence(head, tail, rows):
    tile = head.shape[1]
    if rows % 128:
        index = lax.broadcasted_iota(jnp.int32, (rows, tile), 0)
        ends = (index == head).astype(jnp.float32) - (index == tail).astype(jnp.float32)
        return ends.astype(jnp.bfloat16)
    lane = lax.broadcasted_iota(jnp.int32, (128, tile), 0)
    low_head = (lane == (head & 127)).astype(jnp.bfloat16)
    low_tail = (lane == (tail & 127)).astype(jnp.bfloat16)
    high_head = head >> 7
    high_tail = tail >> 7
    blocks = []
    for block in range(rows // 128):
        on_head = (high_head == block).astype(jnp.bfloat16)
        on_tail = (high_tail == block).astype(jnp.bfloat16)
        blocks.append(low_head * on_head - low_tail * on_tail)
    return jnp.concatenate(blocks, axis=0)


def flow_kernel(scatter):
    def kernel(xs_ref, head_ref, tail_ref, w_ref, *out_ref):
        out_ref, acc = (out_ref[:2], out_ref[2:]) if scatter else (out_ref[0], ())
        step = pl.program_id(0)
        width, rows = xs_ref.shape
        tile = head_ref.shape[1]
        ends = incidence(head_ref[...], tail_ref[...], rows)
        gap = jnp.dot(split3(xs_ref[...]), ends, preferred_element_type=jnp.float32)
        gap = gap[:width] + gap[width:2 * width] + gap[2 * width:]
        if not scatter:
            out_ref[...] = jnp.sum(gap * gap, axis=0, keepdims=True)
            return
        (total,) = acc
        energy_ref = out_ref[1]
        out_ref = out_ref[0]
        weighted = gap * w_ref[...]
        energy = jnp.sum(gap * weighted, axis=1, keepdims=True)
        energy_ref[...] = jnp.where(step == 0, 0.0, energy_ref[...]) + energy
        flow = split3(weighted)
        dims = (((1,), (1,)), ((), ()))
        total[...] = jnp.where(step == 0, 0.0, total[...]) + lax.dot_general(
            flow, ends, dims, preferred_element_type=jnp.float32
        )

        @pl.when(step == pl.num_programs(0) - 1)
        def _():
            sums = total[...]
            out_ref[...] = sums[:width] + sums[width:2 * width] + sums[2 * width:]

    return kernel


def edge_pass(extended, head_rows, tail_slots, weights, scatter):
    width, rows = extended.shape
    edges = head_rows.shape[1]
    tile = edge_tile(rows)
    edge_spec = pl.BlockSpec((1, tile), lambda i: (0, i))
    full = pl.BlockSpec((width, rows), lambda i: (0, 0))
    if scatter:
        out_shape = (jax.ShapeDtypeStruct((width, rows), jnp.float32), jax.ShapeDtypeStruct((width, 1), jnp.float32))
        out_spec = (pl.BlockSpec((width, rows), lambda i: (0, 0)), pl.BlockSpec((width, 1), lambda i: (0, 0)))
        scratch = [pltpu.VMEM((3 * width, rows), jnp.float32)]
    else:
        out_shape = jax.ShapeDtypeStruct((1, edges), jnp.float32)
        out_spec = edge_spec
        scratch = []
    return pl.pallas_call(
        flow_kernel(scatter),
        grid=(edges // tile,),
        in_specs=[full, edge_spec, edge_spec, edge_spec],
        out_specs=out_spec,
        out_shape=out_shape,
        scratch_shapes=scratch,
        compiler_params=pltpu.CompilerParams(
            dimension_semantics=("arbitrary",), vmem_limit_bytes=48 * 1024 * 1024
        ),
    )(extended, head_rows, tail_slots, weights)


def extend(field, halo_rows):
    mirrored = trade(field[:, halo_rows])
    return jnp.concatenate([field, mirrored.reshape(field.shape[0], -1)], axis=1)


def operate(field, shift, head_rows, tail_slots, weights, halo_rows):
    count = field.shape[1]
    width = field.shape[0]
    peers, cap = halo_rows.shape
    extended = extend(field, halo_rows)
    summed, energy = edge_pass(extended, head_rows, tail_slots, weights, True)
    squares = field * field
    own = jnp.stack([jnp.sum(squares, axis=1), jnp.sum(shift * squares, axis=1) + energy[:, 0]], axis=1)
    sent = jnp.concatenate(
        [summed[:, count:].reshape(width, peers, cap), jnp.broadcast_to(own[:, None, :], (width, peers, 2))], axis=2
    )
    got = trade(sent)
    returned = got[:, :, :cap].reshape(width, -1)
    norm, product = jnp.sum(got[:, :, cap:], axis=1).T
    local = summed[:, :count].at[:, halo_rows.reshape(-1)].add(returned)
    return shift * field + local, norm, product, extended[:, count:]


def body(right_side, shift, edge_ends, weights, halo_rows):
    head_rows = edge_ends[0:1]
    tail_slots = edge_ends[1:2]
    weights = weights[None, :]
    share = edge_ends.shape[1] // lax.axis_size("col")
    start = lax.axis_index("col") * share
    quarter = [lax.dynamic_slice_in_dim(item, start, share, axis=1) for item in (head_rows, tail_slots, weights)]
    solution = jnp.zeros_like(right_side)
    residual = right_side
    image, norm_now, product, mirrored = operate(residual, shift, head_rows, tail_slots, weights, halo_rows)
    alpha = norm_now / product
    direction = residual
    along = image
    far_solution = jnp.zeros_like(mirrored)
    far_direction = mirrored
    for step in range(ITERS):
        solution = solution + alpha[:, None] * direction
        far_solution = far_solution + alpha[:, None] * far_direction
        residual = residual - alpha[:, None] * along
        if step + 1 < ITERS:
            image, norm_next, product, mirrored = operate(residual, shift, head_rows, tail_slots, weights, halo_rows)
            ratio = norm_next / norm_now
            alpha = norm_next / (product - ratio * norm_next / alpha)
            direction = residual + ratio[:, None] * direction
            far_direction = mirrored + ratio[:, None] * far_direction
            along = image + ratio[:, None] * along
            norm_now = norm_next
    extended = jnp.concatenate([solution, far_solution], axis=1)
    total = edge_pass(lax.all_gather(extended, "col", axis=0, tiled=True), *quarter, False)[0]
    resistance = lax.all_gather(total, "col", axis=0, tiled=True)
    return (solution, resistance)


def solution(mesh):
    placed = (
        P("col", ("vx", "vy")),
        P(("vx", "vy")),
        P(None, ("vx", "vy")),
        P(("vx", "vy")),
        P(("vx", "vy"), None),
    )
    return jax.shard_map(
        body,
        mesh=mesh,
        in_specs=placed,
        out_specs=(P("col", ("vx", "vy")), P(("vx", "vy"))),
        check_vma=False,
    )
```

```python
import jax
import jax.numpy as jnp
from jax import lax
from jax.experimental import pallas as pl
from jax.experimental.pallas import tpu as pltpu
from jax.sharding import PartitionSpec as P

ITERS = 2


def trade(blocks):
    return lax.all_to_all(blocks, ("vx", "vy"), split_axis=1, concat_axis=1, tiled=True)


def split3(values):
    first = values.astype(jnp.bfloat16)
    rest = values - first.astype(jnp.float32)
    second = rest.astype(jnp.bfloat16)
    third = (rest - second.astype(jnp.float32)).astype(jnp.bfloat16)
    return jnp.concatenate([first, second, third], axis=0)


def edge_tile(rows):
    return 2048 if rows <= 2048 else 256


def incidence(head, tail, rows, local):
    tile = head.shape[1]
    if rows % 128:
        def build(first, size):
            index = lax.broadcasted_iota(jnp.int32, (size, tile), 0) + first
            ends = (index == head).astype(jnp.float32) - (index == tail).astype(jnp.float32)
            return ends.astype(jnp.bfloat16)

        return build
    lane = lax.broadcasted_iota(jnp.int32, (128, tile), 0)
    low_head = (lane == (head & 127)).astype(jnp.bfloat16)
    low_tail = (lane == (tail & 127)).astype(jnp.bfloat16)
    high_head = head >> 7
    high_tail = tail >> 7

    def build(first, size):
        blocks = []
        for block in range(first // 128, (first + size) // 128):
            off_tail = -(high_tail == block).astype(jnp.bfloat16)
            if block * 128 < local:
                on_head = (high_head == block).astype(jnp.bfloat16)
                blocks.append(low_head * on_head + low_tail * off_tail)
            else:
                blocks.append(low_tail * off_tail)
        return jnp.concatenate(blocks, axis=0) if len(blocks) > 1 else blocks[0]

    return build


def pieces(rows):
    step = 256 if rows % 256 == 0 else (128 if rows % 128 == 0 else rows)
    return [(first, step) for first in range(0, rows, step)]


def flow_kernel(scatter, local):
    def kernel(xs_ref, head_ref, tail_ref, w_ref, *out_ref):
        out_ref, acc = (out_ref[:2], out_ref[2:]) if scatter else (out_ref[0], ())
        step = pl.program_id(0)
        width, rows = xs_ref.shape
        head = head_ref[...]
        tail = tail_ref[...]
        xs = split3(xs_ref[...])
        parts = []
        gap = None
        build = incidence(head, tail, rows, local)
        for first, size in pieces(rows):
            ends = build(first, size)
            parts.append(ends)
            term = jnp.dot(xs[:, first:first + size], ends, preferred_element_type=jnp.float32)
            gap = term if gap is None else gap + term
        gap = gap[:width] + gap[width:2 * width] + gap[2 * width:]
        if not scatter:
            out_ref[...] = jnp.sum(gap * gap, axis=0, keepdims=True)
            return
        (total,) = acc
        energy_ref = out_ref[1]
        out_ref = out_ref[0]
        weighted = gap * w_ref[...]
        energy = jnp.sum(gap * weighted, axis=1, keepdims=True)
        energy_ref[...] = jnp.where(step == 0, 0.0, energy_ref[...]) + energy
        flow = split3(weighted)
        dims = (((1,), (1,)), ((), ()))
        for (first, size), ends in zip(pieces(rows), parts):
            window = total[:, first:first + size]
            total[:, first:first + size] = jnp.where(step == 0, 0.0, window) + lax.dot_general(
                flow, ends, dims, preferred_element_type=jnp.float32
            )

        @pl.when(step == pl.num_programs(0) - 1)
        def _():
            sums = total[...]
            out_ref[...] = sums[:width] + sums[width:2 * width] + sums[2 * width:]

    return kernel


def edge_pass(extended, head_rows, tail_slots, weights, scatter, local):
    width, rows = extended.shape
    edges = head_rows.shape[1]
    tile = edge_tile(rows)
    edge_spec = pl.BlockSpec((1, tile), lambda i: (0, i))
    full = pl.BlockSpec((width, rows), lambda i: (0, 0))
    if scatter:
        out_shape = (jax.ShapeDtypeStruct((width, rows), jnp.float32), jax.ShapeDtypeStruct((width, 1), jnp.float32))
        out_spec = (pl.BlockSpec((width, rows), lambda i: (0, 0)), pl.BlockSpec((width, 1), lambda i: (0, 0)))
        scratch = [pltpu.VMEM((3 * width, rows), jnp.float32)]
    else:
        out_shape = jax.ShapeDtypeStruct((1, edges), jnp.float32)
        out_spec = edge_spec
        scratch = []
    return pl.pallas_call(
        flow_kernel(scatter, local),
        grid=(edges // tile,),
        in_specs=[full, edge_spec, edge_spec, edge_spec],
        out_specs=out_spec,
        out_shape=out_shape,
        scratch_shapes=scratch,
        compiler_params=pltpu.CompilerParams(
            dimension_semantics=("arbitrary",), vmem_limit_bytes=48 * 1024 * 1024
        ),
    )(extended, head_rows, tail_slots, weights)


def extend(field, halo_rows):
    mirrored = trade(field[:, halo_rows])
    return jnp.concatenate([field, mirrored.reshape(field.shape[0], -1)], axis=1)


def operate(field, shift, head_rows, tail_slots, weights, halo_rows):
    count = field.shape[1]
    width = field.shape[0]
    peers, cap = halo_rows.shape
    extended = extend(field, halo_rows)
    summed, energy = edge_pass(extended, head_rows, tail_slots, weights, True, count)
    squares = field * field
    own = jnp.stack([jnp.sum(squares, axis=1), jnp.sum(shift * squares, axis=1) + energy[:, 0]], axis=1)
    sent = jnp.concatenate(
        [summed[:, count:].reshape(width, peers, cap), jnp.broadcast_to(own[:, None, :], (width, peers, 2))], axis=2
    )
    got = trade(sent)
    returned = got[:, :, :cap].reshape(width, -1)
    norm, product = jnp.sum(got[:, :, cap:], axis=1).T
    local = summed[:, :count].at[:, halo_rows.reshape(-1)].add(returned)
    return shift * field + local, norm, product, extended[:, count:]


def body(right_side, shift, edge_ends, weights, halo_rows):
    head_rows = edge_ends[0:1]
    tail_slots = edge_ends[1:2]
    weights = weights[None, :]
    share = edge_ends.shape[1] // lax.axis_size("col")
    start = lax.axis_index("col") * share
    quarter = [lax.dynamic_slice_in_dim(item, start, share, axis=1) for item in (head_rows, tail_slots, weights)]
    solution = jnp.zeros_like(right_side)
    residual = right_side
    image, norm_now, product, mirrored = operate(residual, shift, head_rows, tail_slots, weights, halo_rows)
    alpha = norm_now / product
    direction = residual
    along = image
    far_solution = jnp.zeros_like(mirrored)
    far_direction = mirrored
    for step in range(ITERS):
        solution = solution + alpha[:, None] * direction
        far_solution = far_solution + alpha[:, None] * far_direction
        residual = residual - alpha[:, None] * along
        if step + 1 < ITERS:
            image, norm_next, product, mirrored = operate(residual, shift, head_rows, tail_slots, weights, halo_rows)
            ratio = norm_next / norm_now
            alpha = norm_next / (product - ratio * norm_next / alpha)
            direction = residual + ratio[:, None] * direction
            far_direction = mirrored + ratio[:, None] * far_direction
            along = image + ratio[:, None] * along
            norm_now = norm_next
    extended = jnp.concatenate([solution, far_solution], axis=1)
    total = edge_pass(lax.all_gather(extended, "col", axis=0, tiled=True), *quarter, False, solution.shape[1])[0]
    resistance = lax.all_gather(total, "col", axis=0, tiled=True)
    return (solution, resistance)


def solution(mesh):
    placed = (
        P("col", ("vx", "vy")),
        P(("vx", "vy")),
        P(None, ("vx", "vy")),
        P(("vx", "vy")),
        P(("vx", "vy"), None),
    )
    return jax.shard_map(
        body,
        mesh=mesh,
        in_specs=placed,
        out_specs=(P("col", ("vx", "vy")), P(("vx", "vy"))),
        check_vma=False,
    )
```

```python
import jax
import jax.numpy as jnp
from jax import lax
from jax.experimental import pallas as pl
from jax.experimental.pallas import tpu as pltpu
from jax.sharding import PartitionSpec as P

ITERS = 2


def trade(blocks):
    axes = ("vx", "vy")
    count = blocks.shape[1]
    if count > 8:
        return lax.all_to_all(blocks, axes, split_axis=1, concat_axis=1, tiled=True)
    me = lax.axis_index(axes)
    got = [lax.dynamic_slice_in_dim(blocks, me, 1, axis=1)]
    for shift in range(1, count):
        send = lax.dynamic_slice_in_dim(blocks, (me + shift) % count, 1, axis=1)
        got.append(lax.ppermute(send, axes, [(i, (i + shift) % count) for i in range(count)]))
    stacked = jnp.concatenate(got, axis=1)
    order = (me - jnp.arange(count)) % count
    return jnp.take(stacked, order, axis=1)


def split3(values):
    first = values.astype(jnp.bfloat16)
    rest = values - first.astype(jnp.float32)
    second = rest.astype(jnp.bfloat16)
    third = (rest - second.astype(jnp.float32)).astype(jnp.bfloat16)
    return jnp.concatenate([first, second, third], axis=0)


def edge_tile(rows):
    return 2048 if rows <= 2048 else 256


def incidence(head, tail, rows, local):
    tile = head.shape[1]
    if rows % 128:
        def build(first, size):
            index = lax.broadcasted_iota(jnp.int32, (size, tile), 0) + first
            ends = (index == head).astype(jnp.float32) - (index == tail).astype(jnp.float32)
            return ends.astype(jnp.bfloat16)

        return build
    lane = lax.broadcasted_iota(jnp.int32, (128, tile), 0)
    low_head = (lane == (head & 127)).astype(jnp.bfloat16)
    low_tail = (lane == (tail & 127)).astype(jnp.bfloat16)
    high_head = head >> 7
    high_tail = tail >> 7

    def build(first, size):
        blocks = []
        for block in range(first // 128, (first + size) // 128):
            off_tail = -(high_tail == block).astype(jnp.bfloat16)
            if block * 128 < local:
                on_head = (high_head == block).astype(jnp.bfloat16)
                blocks.append(low_head * on_head + low_tail * off_tail)
            else:
                blocks.append(low_tail * off_tail)
        return jnp.concatenate(blocks, axis=0) if len(blocks) > 1 else blocks[0]

    return build


def pieces(rows):
    step = 256 if rows % 256 == 0 else (128 if rows % 128 == 0 else rows)
    return [(first, step) for first in range(0, rows, step)]


def flow_kernel(scatter, local):
    def kernel(xs_ref, head_ref, tail_ref, w_ref, *out_ref):
        out_ref, acc = (out_ref[:2], out_ref[2:]) if scatter else (out_ref[0], ())
        step = pl.program_id(0)
        width, rows = xs_ref.shape
        head = head_ref[...]
        tail = tail_ref[...]
        xs = split3(xs_ref[...])
        parts = []
        gap = None
        build = incidence(head, tail, rows, local)
        for first, size in pieces(rows):
            ends = build(first, size)
            parts.append(ends)
            term = jnp.dot(xs[:, first:first + size], ends, preferred_element_type=jnp.float32)
            gap = term if gap is None else gap + term
        gap = gap[:width] + gap[width:2 * width] + gap[2 * width:]
        if not scatter:
            out_ref[...] = jnp.sum(gap * gap, axis=0, keepdims=True)
            return
        (total,) = acc
        energy_ref = out_ref[1]
        out_ref = out_ref[0]
        weighted = gap * w_ref[...]
        energy = jnp.sum(gap * weighted, axis=1, keepdims=True)
        energy_ref[...] = jnp.where(step == 0, 0.0, energy_ref[...]) + energy
        flow = split3(weighted)
        dims = (((1,), (1,)), ((), ()))
        for (first, size), ends in zip(pieces(rows), parts):
            window = total[:, first:first + size]
            total[:, first:first + size] = jnp.where(step == 0, 0.0, window) + lax.dot_general(
                flow, ends, dims, preferred_element_type=jnp.float32
            )

        @pl.when(step == pl.num_programs(0) - 1)
        def _():
            sums = total[...]
            out_ref[...] = sums[:width] + sums[width:2 * width] + sums[2 * width:]

    return kernel


def edge_pass(extended, head_rows, tail_slots, weights, scatter, local):
    width, rows = extended.shape
    edges = head_rows.shape[1]
    tile = edge_tile(rows)
    edge_spec = pl.BlockSpec((1, tile), lambda i: (0, i))
    full = pl.BlockSpec((width, rows), lambda i: (0, 0))
    if scatter:
        out_shape = (jax.ShapeDtypeStruct((width, rows), jnp.float32), jax.ShapeDtypeStruct((width, 1), jnp.float32))
        out_spec = (pl.BlockSpec((width, rows), lambda i: (0, 0)), pl.BlockSpec((width, 1), lambda i: (0, 0)))
        scratch = [pltpu.VMEM((3 * width, rows), jnp.float32)]
    else:
        out_shape = jax.ShapeDtypeStruct((1, edges), jnp.float32)
        out_spec = edge_spec
        scratch = []
    return pl.pallas_call(
        flow_kernel(scatter, local),
        grid=(edges // tile,),
        in_specs=[full, edge_spec, edge_spec, edge_spec],
        out_specs=out_spec,
        out_shape=out_shape,
        scratch_shapes=scratch,
        compiler_params=pltpu.CompilerParams(
            dimension_semantics=("arbitrary",), vmem_limit_bytes=48 * 1024 * 1024
        ),
    )(extended, head_rows, tail_slots, weights)


def extend(field, halo_rows):
    mirrored = trade(field[:, halo_rows])
    return jnp.concatenate([field, mirrored.reshape(field.shape[0], -1)], axis=1)


def operate(field, shift, head_rows, tail_slots, weights, halo_rows):
    count = field.shape[1]
    width = field.shape[0]
    peers, cap = halo_rows.shape
    extended = extend(field, halo_rows)
    summed, energy = edge_pass(extended, head_rows, tail_slots, weights, True, count)
    squares = field * field
    own = jnp.stack([jnp.sum(squares, axis=1), jnp.sum(shift * squares, axis=1) + energy[:, 0]], axis=1)
    sent = jnp.concatenate(
        [summed[:, count:].reshape(width, peers, cap), jnp.broadcast_to(own[:, None, :], (width, peers, 2))], axis=2
    )
    got = trade(sent)
    returned = got[:, :, :cap].reshape(width, -1)
    norm, product = jnp.sum(got[:, :, cap:], axis=1).T
    local = summed[:, :count].at[:, halo_rows.reshape(-1)].add(returned)
    return shift * field + local, norm, product, extended[:, count:]


def body(right_side, shift, edge_ends, weights, halo_rows):
    head_rows = edge_ends[0:1]
    tail_slots = edge_ends[1:2]
    weights = weights[None, :]
    share = edge_ends.shape[1] // lax.axis_size("col")
    start = lax.axis_index("col") * share
    quarter = [lax.dynamic_slice_in_dim(item, start, share, axis=1) for item in (head_rows, tail_slots, weights)]
    solution = jnp.zeros_like(right_side)
    residual = right_side
    image, norm_now, product, mirrored = operate(residual, shift, head_rows, tail_slots, weights, halo_rows)
    alpha = norm_now / product
    direction = residual
    along = image
    far_solution = jnp.zeros_like(mirrored)
    far_direction = mirrored
    for step in range(ITERS):
        solution = solution + alpha[:, None] * direction
        far_solution = far_solution + alpha[:, None] * far_direction
        residual = residual - alpha[:, None] * along
        if step + 1 < ITERS:
            image, norm_next, product, mirrored = operate(residual, shift, head_rows, tail_slots, weights, halo_rows)
            ratio = norm_next / norm_now
            alpha = norm_next / (product - ratio * norm_next / alpha)
            direction = residual + ratio[:, None] * direction
            far_direction = mirrored + ratio[:, None] * far_direction
            along = image + ratio[:, None] * along
            norm_now = norm_next
    extended = jnp.concatenate([solution, far_solution], axis=1)
    total = edge_pass(lax.all_gather(extended, "col", axis=0, tiled=True), *quarter, False, solution.shape[1])[0]
    resistance = lax.all_gather(total, "col", axis=0, tiled=True)
    return (solution, resistance)


def solution(mesh):
    placed = (
        P("col", ("vx", "vy")),
        P(("vx", "vy")),
        P(None, ("vx", "vy")),
        P(("vx", "vy")),
        P(("vx", "vy"), None),
    )
    return jax.shard_map(
        body,
        mesh=mesh,
        in_specs=placed,
        out_specs=(P("col", ("vx", "vy")), P(("vx", "vy"))),
        check_vma=False,
    )
```

```python
import jax
import jax.numpy as jnp
from jax import lax
from jax.experimental import pallas as pl
from jax.experimental.pallas import tpu as pltpu
from jax.sharding import PartitionSpec as P

ITERS = 2


def trade(blocks):
    return lax.all_to_all(blocks, ("vx", "vy"), split_axis=1, concat_axis=1, tiled=True)


def split3(values):
    first = values.astype(jnp.bfloat16)
    rest = values - first.astype(jnp.float32)
    second = rest.astype(jnp.bfloat16)
    third = (rest - second.astype(jnp.float32)).astype(jnp.bfloat16)
    return jnp.concatenate([first, second, third], axis=0)


def edge_tile(rows):
    return 2048 if rows <= 2048 else 256


def incidence(head, tail, rows, local):
    tile = head.shape[1]
    if rows % 128:
        def build(first, size):
            index = lax.broadcasted_iota(jnp.int32, (size, tile), 0) + first
            ends = (index == head).astype(jnp.float32) - (index == tail).astype(jnp.float32)
            return ends.astype(jnp.bfloat16)

        return build
    lane = lax.broadcasted_iota(jnp.int32, (128, tile), 0)
    low_head = (lane == (head & 127)).astype(jnp.bfloat16)
    low_tail = (lane == (tail & 127)).astype(jnp.bfloat16)
    high_head = head >> 7
    high_tail = tail >> 7

    def build(first, size):
        blocks = []
        for block in range(first // 128, (first + size) // 128):
            off_tail = -(high_tail == block).astype(jnp.bfloat16)
            if block * 128 < local:
                on_head = (high_head == block).astype(jnp.bfloat16)
                blocks.append(low_head * on_head + low_tail * off_tail)
            else:
                blocks.append(low_tail * off_tail)
        return jnp.concatenate(blocks, axis=0) if len(blocks) > 1 else blocks[0]

    return build


def pieces(rows):
    step = 256 if rows % 256 == 0 else (128 if rows % 128 == 0 else rows)
    return [(first, step) for first in range(0, rows, step)]


def flow_kernel(mode, local):
    scatter = mode == "scatter"

    def kernel(xs_ref, head_ref, tail_ref, w_ref, *out_ref):
        out_ref, acc = (out_ref[:2], out_ref[2:]) if scatter else (out_ref[0], ())
        step = pl.program_id(0)
        width, rows = xs_ref.shape
        head = head_ref[...]
        tail = tail_ref[...]
        xs = split3(xs_ref[...])
        parts = []
        gap = None
        build = incidence(head, tail, rows, local)
        for first, size in pieces(rows):
            ends = build(first, size)
            parts.append(ends)
            term = jnp.dot(xs[:, first:first + size], ends, preferred_element_type=jnp.float32)
            gap = term if gap is None else gap + term
        gap = gap[:width] + gap[width:2 * width] + gap[2 * width:]
        if mode == "gap":
            out_ref[...] = jnp.sum(gap * gap, axis=0, keepdims=True)
            return
        weighted = gap * w_ref[...]
        energy = jnp.sum(gap * weighted, axis=1, keepdims=True)
        if mode == "energy":
            out_ref[...] = jnp.where(step == 0, 0.0, out_ref[...]) + energy
            return
        (total,) = acc
        energy_ref = out_ref[1]
        out_ref = out_ref[0]
        energy_ref[...] = jnp.where(step == 0, 0.0, energy_ref[...]) + energy
        flow = split3(weighted)
        dims = (((1,), (1,)), ((), ()))
        for (first, size), ends in zip(pieces(rows), parts):
            window = total[:, first:first + size]
            total[:, first:first + size] = jnp.where(step == 0, 0.0, window) + lax.dot_general(
                flow, ends, dims, preferred_element_type=jnp.float32
            )

        @pl.when(step == pl.num_programs(0) - 1)
        def _():
            sums = total[...]
            out_ref[...] = sums[:width] + sums[width:2 * width] + sums[2 * width:]

    return kernel


def edge_pass(extended, head_rows, tail_slots, weights, mode, local):
    width, rows = extended.shape
    edges = head_rows.shape[1]
    tile = edge_tile(rows)
    edge_spec = pl.BlockSpec((1, tile), lambda i: (0, i))
    full = pl.BlockSpec((width, rows), lambda i: (0, 0))
    if mode == "scatter":
        out_shape = (jax.ShapeDtypeStruct((width, rows), jnp.float32), jax.ShapeDtypeStruct((width, 1), jnp.float32))
        out_spec = (pl.BlockSpec((width, rows), lambda i: (0, 0)), pl.BlockSpec((width, 1), lambda i: (0, 0)))
        scratch = [pltpu.VMEM((3 * width, rows), jnp.float32)]
    elif mode == "energy":
        out_shape = jax.ShapeDtypeStruct((width, 1), jnp.float32)
        out_spec = pl.BlockSpec((width, 1), lambda i: (0, 0))
        scratch = []
    else:
        out_shape = jax.ShapeDtypeStruct((1, edges), jnp.float32)
        out_spec = edge_spec
        scratch = []
    return pl.pallas_call(
        flow_kernel(mode, local),
        grid=(edges // tile,),
        in_specs=[full, edge_spec, edge_spec, edge_spec],
        out_specs=out_spec,
        out_shape=out_shape,
        scratch_shapes=scratch,
        compiler_params=pltpu.CompilerParams(
            dimension_semantics=("arbitrary",), vmem_limit_bytes=48 * 1024 * 1024
        ),
    )(extended, head_rows, tail_slots, weights)


def extend(field, halo_rows):
    mirrored = trade(field[:, halo_rows])
    return jnp.concatenate([field, mirrored.reshape(field.shape[0], -1)], axis=1)


def operate(field, shift, head_rows, tail_slots, weights, halo_rows, full=True):
    count = field.shape[1]
    width = field.shape[0]
    peers, cap = halo_rows.shape
    extended = extend(field, halo_rows)
    squares = field * field
    if not full:
        energy = edge_pass(extended, head_rows, tail_slots, weights, "energy", count)
        own = jnp.stack([jnp.sum(squares, axis=1), jnp.sum(shift * squares, axis=1) + energy[:, 0]], axis=1)
        got = trade(jnp.broadcast_to(own[:, None, :], (width, peers, 2)))
        norm, product = jnp.sum(got, axis=1).T
        return None, norm, product, extended[:, count:]
    summed, energy = edge_pass(extended, head_rows, tail_slots, weights, "scatter", count)
    own = jnp.stack([jnp.sum(squares, axis=1), jnp.sum(shift * squares, axis=1) + energy[:, 0]], axis=1)
    sent = jnp.concatenate(
        [summed[:, count:].reshape(width, peers, cap), jnp.broadcast_to(own[:, None, :], (width, peers, 2))], axis=2
    )
    got = trade(sent)
    returned = got[:, :, :cap].reshape(width, -1)
    norm, product = jnp.sum(got[:, :, cap:], axis=1).T
    local = summed[:, :count].at[:, halo_rows.reshape(-1)].add(returned)
    return shift * field + local, norm, product, extended[:, count:]


def body(right_side, shift, edge_ends, weights, halo_rows):
    head_rows = edge_ends[0:1]
    tail_slots = edge_ends[1:2]
    weights = weights[None, :]
    share = edge_ends.shape[1] // lax.axis_size("col")
    start = lax.axis_index("col") * share
    quarter = [lax.dynamic_slice_in_dim(item, start, share, axis=1) for item in (head_rows, tail_slots, weights)]
    solution = jnp.zeros_like(right_side)
    residual = right_side
    image, norm_now, product, mirrored = operate(residual, shift, head_rows, tail_slots, weights, halo_rows)
    alpha = norm_now / product
    direction = residual
    along = image
    far_solution = jnp.zeros_like(mirrored)
    far_direction = mirrored
    for step in range(ITERS):
        solution = solution + alpha[:, None] * direction
        far_solution = far_solution + alpha[:, None] * far_direction
        residual = None if along is None else residual - alpha[:, None] * along
        if step + 1 < ITERS:
            image, norm_next, product, mirrored = operate(
                residual, shift, head_rows, tail_slots, weights, halo_rows, step + 2 < ITERS
            )
            ratio = norm_next / norm_now
            alpha = norm_next / (product - ratio * norm_next / alpha)
            direction = residual + ratio[:, None] * direction
            far_direction = mirrored + ratio[:, None] * far_direction
            along = None if image is None else image + ratio[:, None] * along
            norm_now = norm_next
    extended = jnp.concatenate([solution, far_solution], axis=1)
    total = edge_pass(lax.all_gather(extended, "col", axis=0, tiled=True), *quarter, "gap", solution.shape[1])[0]
    resistance = lax.all_gather(total, "col", axis=0, tiled=True)
    return (solution, resistance)


def solution(mesh):
    placed = (
        P("col", ("vx", "vy")),
        P(("vx", "vy")),
        P(None, ("vx", "vy")),
        P(("vx", "vy")),
        P(("vx", "vy"), None),
    )
    return jax.shard_map(
        body,
        mesh=mesh,
        in_specs=placed,
        out_specs=(P("col", ("vx", "vy")), P(("vx", "vy"))),
        check_vma=False,
    )
```

```python
import jax
import jax.numpy as jnp
from jax import lax
from jax.experimental import pallas as pl
from jax.experimental.pallas import tpu as pltpu
from jax.sharding import PartitionSpec as P

ITERS = 2


def trade(blocks):
    return lax.all_to_all(blocks, ("vx", "vy"), split_axis=1, concat_axis=1, tiled=True)


def split3(values):
    first = values.astype(jnp.bfloat16)
    rest = values - first.astype(jnp.float32)
    second = rest.astype(jnp.bfloat16)
    third = (rest - second.astype(jnp.float32)).astype(jnp.bfloat16)
    return jnp.concatenate([first, second, third], axis=0)


def edge_tile(rows):
    return 2048 if rows <= 2048 else 256


def incidence(head, tail, rows, local):
    tile = head.shape[1]
    if rows % 128:
        def build(first, size):
            index = lax.broadcasted_iota(jnp.int32, (size, tile), 0) + first
            ends = (index == head).astype(jnp.float32) - (index == tail).astype(jnp.float32)
            return ends.astype(jnp.bfloat16)

        return build
    lane = lax.broadcasted_iota(jnp.int32, (128, tile), 0)
    low_head = (lane == (head & 127)).astype(jnp.bfloat16)
    low_tail = (lane == (tail & 127)).astype(jnp.bfloat16)
    high_head = head >> 7
    high_tail = tail >> 7

    def build(first, size):
        blocks = []
        for block in range(first // 128, (first + size) // 128):
            off_tail = -(high_tail == block).astype(jnp.bfloat16)
            if block * 128 < local:
                on_head = (high_head == block).astype(jnp.bfloat16)
                blocks.append(low_head * on_head + low_tail * off_tail)
            else:
                blocks.append(low_tail * off_tail)
        return jnp.concatenate(blocks, axis=0) if len(blocks) > 1 else blocks[0]

    return build


def pieces(rows):
    step = 256 if rows % 256 == 0 else (128 if rows % 128 == 0 else rows)
    return [(first, step) for first in range(0, rows, step)]


def flow_kernel(mode, local):
    scatter = mode == "scatter"

    def kernel(xs_ref, head_ref, tail_ref, w_ref, *out_ref):
        out_ref, acc = (out_ref[:2], out_ref[2:]) if scatter else (out_ref[0], ())
        step = pl.program_id(0)
        width, rows = xs_ref.shape
        head = head_ref[...]
        tail = tail_ref[...]
        xs = split3(xs_ref[...])
        parts = []
        gap = None
        build = incidence(head, tail, rows, local)
        for first, size in pieces(rows):
            ends = build(first, size)
            parts.append(ends)
            term = jnp.dot(xs[:, first:first + size], ends, preferred_element_type=jnp.float32)
            gap = term if gap is None else gap + term
        gap = gap[:width] + gap[width:2 * width] + gap[2 * width:]
        if mode == "gap":
            out_ref[...] = jnp.sum(gap * gap, axis=0, keepdims=True)
            return
        weighted = gap * w_ref[...]
        energy = jnp.sum(gap * weighted, axis=1, keepdims=True)
        if mode == "energy":
            out_ref[...] = jnp.where(step == 0, 0.0, out_ref[...]) + energy
            return
        (total,) = acc
        energy_ref = out_ref[1]
        out_ref = out_ref[0]
        energy_ref[...] = jnp.where(step == 0, 0.0, energy_ref[...]) + energy
        flow = split3(weighted)
        dims = (((1,), (1,)), ((), ()))
        for (first, size), ends in zip(pieces(rows), parts):
            window = total[:, first:first + size]
            total[:, first:first + size] = jnp.where(step == 0, 0.0, window) + lax.dot_general(
                flow, ends, dims, preferred_element_type=jnp.float32
            )

        @pl.when(step == pl.num_programs(0) - 1)
        def _():
            sums = total[...]
            out_ref[...] = sums[:width] + sums[width:2 * width] + sums[2 * width:]

    return kernel


def edge_pass(extended, head_rows, tail_slots, weights, mode, local):
    width, rows = extended.shape
    edges = head_rows.shape[1]
    tile = edge_tile(rows)
    edge_spec = pl.BlockSpec((1, tile), lambda i: (0, i))
    full = pl.BlockSpec((width, rows), lambda i: (0, 0))
    if mode == "scatter":
        out_shape = (jax.ShapeDtypeStruct((width, rows), jnp.float32), jax.ShapeDtypeStruct((width, 1), jnp.float32))
        out_spec = (pl.BlockSpec((width, rows), lambda i: (0, 0)), pl.BlockSpec((width, 1), lambda i: (0, 0)))
        scratch = [pltpu.VMEM((3 * width, rows), jnp.float32)]
    elif mode == "energy":
        out_shape = jax.ShapeDtypeStruct((width, 1), jnp.float32)
        out_spec = pl.BlockSpec((width, 1), lambda i: (0, 0))
        scratch = []
    else:
        out_shape = jax.ShapeDtypeStruct((1, edges), jnp.float32)
        out_spec = edge_spec
        scratch = []
    return pl.pallas_call(
        flow_kernel(mode, local),
        grid=(edges // tile,),
        in_specs=[full, edge_spec, edge_spec, edge_spec],
        out_specs=out_spec,
        out_shape=out_shape,
        scratch_shapes=scratch,
        compiler_params=pltpu.CompilerParams(
            dimension_semantics=("arbitrary",), vmem_limit_bytes=48 * 1024 * 1024
        ),
    )(extended, head_rows, tail_slots, weights)


def extend(field, halo_rows):
    mirrored = trade(field[:, halo_rows])
    return jnp.concatenate([field, mirrored.reshape(field.shape[0], -1)], axis=1)


def operate(field, shift, head_rows, tail_slots, weights, halo_rows, full=True):
    count = field.shape[1]
    width = field.shape[0]
    peers, cap = halo_rows.shape
    extended = extend(field, halo_rows)
    squares = field * field
    if not full:
        energy = edge_pass(extended, head_rows, tail_slots, weights, "energy", count)
        own = jnp.stack([jnp.sum(squares, axis=1), jnp.sum(shift * squares, axis=1) + energy[:, 0]], axis=1)
        return None, own, None, extended
    summed, energy = edge_pass(extended, head_rows, tail_slots, weights, "scatter", count)
    own = jnp.stack([jnp.sum(squares, axis=1), jnp.sum(shift * squares, axis=1) + energy[:, 0]], axis=1)
    sent = jnp.concatenate(
        [summed[:, count:].reshape(width, peers, cap), jnp.broadcast_to(own[:, None, :], (width, peers, 2))], axis=2
    )
    got = trade(sent)
    returned = got[:, :, :cap].reshape(width, -1)
    norm, product = jnp.sum(got[:, :, cap:], axis=1).T
    local = summed[:, :count].at[:, halo_rows.reshape(-1)].add(returned)
    return shift * field + local, norm, product, extended


def body(right_side, shift, edge_ends, weights, halo_rows):
    head_rows = edge_ends[0:1]
    tail_slots = edge_ends[1:2]
    weights = weights[None, :]
    share = edge_ends.shape[1] // lax.axis_size("col")
    start = lax.axis_index("col") * share
    quarter = [lax.dynamic_slice_in_dim(item, start, share, axis=1) for item in (head_rows, tail_slots, weights)]
    residual = right_side
    image, norm_now, product, first_ext = operate(residual, shift, head_rows, tail_slots, weights, halo_rows)
    first_all = lax.all_gather(first_ext, "col", axis=0, tiled=True)
    alpha = norm_now / product
    residual = residual - alpha[:, None] * image
    _, own, _, second_ext = operate(residual, shift, head_rows, tail_slots, weights, halo_rows, False)
    second_all = lax.all_gather(second_ext, "col", axis=0, tiled=True)
    stats = jnp.concatenate([own, alpha[:, None], norm_now[:, None]], axis=1)
    stats = lax.all_gather(stats, ("vx", "vy", "col"), axis=0, tiled=False)
    parts = lax.axis_size(("vx", "vy"))
    stats = stats.reshape(parts, -1, stats.shape[-1])
    norm_next = jnp.sum(stats[:, :, 0], axis=0)
    product = jnp.sum(stats[:, :, 1], axis=0)
    alpha_all = stats[0, :, 2]
    ratio = norm_next / stats[0, :, 3]
    alpha_next = norm_next / (product - ratio * norm_next / alpha_all)
    lead = alpha_all + alpha_next * ratio
    width = right_side.shape[0]
    mine = lax.axis_index("col") * width
    own_lead = lax.dynamic_slice_in_dim(lead, mine, width)
    own_next = lax.dynamic_slice_in_dim(alpha_next, mine, width)
    solution = own_lead[:, None] * right_side + own_next[:, None] * residual
    extended = lead[:, None] * first_all + alpha_next[:, None] * second_all
    total = edge_pass(extended, *quarter, "gap", right_side.shape[1])[0]
    resistance = lax.all_gather(total, "col", axis=0, tiled=True)
    return (solution, resistance)


def solution(mesh):
    placed = (
        P("col", ("vx", "vy")),
        P(("vx", "vy")),
        P(None, ("vx", "vy")),
        P(("vx", "vy")),
        P(("vx", "vy"), None),
    )
    return jax.shard_map(
        body,
        mesh=mesh,
        in_specs=placed,
        out_specs=(P("col", ("vx", "vy")), P(("vx", "vy"))),
        check_vma=False,
    )
```

```python
import jax
import jax.numpy as jnp
from jax import lax
from jax.experimental import pallas as pl
from jax.experimental.pallas import tpu as pltpu
from jax.sharding import PartitionSpec as P

ITERS = 2


def trade(blocks):
    return lax.all_to_all(blocks, ("vx", "vy"), split_axis=1, concat_axis=1, tiled=True)


def split3(values):
    first = values.astype(jnp.bfloat16)
    rest = values - first.astype(jnp.float32)
    second = rest.astype(jnp.bfloat16)
    third = (rest - second.astype(jnp.float32)).astype(jnp.bfloat16)
    return jnp.concatenate([first, second, third], axis=0)


def edge_tile(rows):
    return 2048 if rows <= 2048 else 256


def incidence(head, tail, rows, local):
    tile = head.shape[1]
    if rows % 128:
        def build(first, size):
            index = lax.broadcasted_iota(jnp.int32, (size, tile), 0) + first
            ends = (index == head).astype(jnp.float32) - (index == tail).astype(jnp.float32)
            return ends.astype(jnp.bfloat16)

        return build
    lane = lax.broadcasted_iota(jnp.int32, (128, tile), 0)
    low_head = (lane == (head & 127)).astype(jnp.bfloat16)
    low_tail = (lane == (tail & 127)).astype(jnp.bfloat16)
    high_head = head >> 7
    high_tail = tail >> 7

    def build(first, size):
        blocks = []
        for block in range(first // 128, (first + size) // 128):
            off_tail = -(high_tail == block).astype(jnp.bfloat16)
            if block * 128 < local:
                on_head = (high_head == block).astype(jnp.bfloat16)
                blocks.append(low_head * on_head + low_tail * off_tail)
            else:
                blocks.append(low_tail * off_tail)
        return jnp.concatenate(blocks, axis=0) if len(blocks) > 1 else blocks[0]

    return build


def pieces(rows):
    step = 256 if rows % 256 == 0 else (128 if rows % 128 == 0 else rows)
    return [(first, step) for first in range(0, rows, step)]


def flow_kernel(mode, local):
    scatter = mode == "scatter"

    def kernel(xs_ref, head_ref, tail_ref, w_ref, *out_ref):
        out_ref, acc = (out_ref[:2], out_ref[2:]) if scatter else (out_ref[0], ())
        step = pl.program_id(0)
        width, rows = xs_ref.shape
        head = head_ref[...]
        tail = tail_ref[...]
        xs = split3(xs_ref[...])
        parts = []
        gap = None
        build = incidence(head, tail, rows, local)
        for first, size in pieces(rows):
            ends = build(first, size)
            parts.append(ends)
            term = jnp.dot(xs[:, first:first + size], ends, preferred_element_type=jnp.float32)
            gap = term if gap is None else gap + term
        gap = gap[:width] + gap[width:2 * width] + gap[2 * width:]
        if mode == "gap":
            out_ref[...] = jnp.sum(gap * gap, axis=0, keepdims=True)
            return
        weighted = gap * w_ref[...]
        energy = jnp.sum(gap * weighted, axis=1, keepdims=True)
        if mode == "energy":
            out_ref[...] = jnp.where(step == 0, 0.0, out_ref[...]) + energy
            return
        (total,) = acc
        energy_ref = out_ref[1]
        out_ref = out_ref[0]
        energy_ref[...] = jnp.where(step == 0, 0.0, energy_ref[...]) + energy
        flow = split3(weighted)
        dims = (((1,), (1,)), ((), ()))
        for (first, size), ends in zip(pieces(rows), parts):
            window = total[:, first:first + size]
            total[:, first:first + size] = jnp.where(step == 0, 0.0, window) + lax.dot_general(
                flow, ends, dims, preferred_element_type=jnp.float32
            )

        @pl.when(step == pl.num_programs(0) - 1)
        def _():
            sums = total[...]
            out_ref[...] = sums[:width] + sums[width:2 * width] + sums[2 * width:]

    return kernel


def edge_pass(extended, head_rows, tail_slots, weights, mode, local):
    width, rows = extended.shape
    edges = head_rows.shape[1]
    tile = edge_tile(rows)
    edge_spec = pl.BlockSpec((1, tile), lambda i: (0, i))
    full = pl.BlockSpec((width, rows), lambda i: (0, 0))
    if mode == "scatter":
        out_shape = (jax.ShapeDtypeStruct((width, rows), jnp.float32), jax.ShapeDtypeStruct((width, 1), jnp.float32))
        out_spec = (pl.BlockSpec((width, rows), lambda i: (0, 0)), pl.BlockSpec((width, 1), lambda i: (0, 0)))
        scratch = [pltpu.VMEM((3 * width, rows), jnp.float32)]
    elif mode == "energy":
        out_shape = jax.ShapeDtypeStruct((width, 1), jnp.float32)
        out_spec = pl.BlockSpec((width, 1), lambda i: (0, 0))
        scratch = []
    else:
        out_shape = jax.ShapeDtypeStruct((1, edges), jnp.float32)
        out_spec = edge_spec
        scratch = []
    return pl.pallas_call(
        flow_kernel(mode, local),
        grid=(edges // tile,),
        in_specs=[full, edge_spec, edge_spec, edge_spec],
        out_specs=out_spec,
        out_shape=out_shape,
        scratch_shapes=scratch,
        compiler_params=pltpu.CompilerParams(
            dimension_semantics=("arbitrary",), vmem_limit_bytes=48 * 1024 * 1024
        ),
    )(extended, head_rows, tail_slots, weights)


def picker(halo_rows, count):
    flat = halo_rows.reshape(-1, 1)
    return (flat == lax.broadcasted_iota(jnp.int32, (flat.shape[0], count), 1)).astype(jnp.float32)


def extend(field, halo_rows):
    peers, cap = halo_rows.shape
    chosen = jnp.dot(field, picker(halo_rows, field.shape[1]).T, precision=lax.Precision.HIGHEST)
    mirrored = trade(chosen.reshape(field.shape[0], peers, cap))
    return jnp.concatenate([field, mirrored.reshape(field.shape[0], -1)], axis=1)


def operate(field, shift, head_rows, tail_slots, weights, halo_rows, full=True):
    count = field.shape[1]
    width = field.shape[0]
    peers, cap = halo_rows.shape
    extended = extend(field, halo_rows)
    squares = field * field
    if not full:
        energy = edge_pass(extended, head_rows, tail_slots, weights, "energy", count)
        own = jnp.stack([jnp.sum(squares, axis=1), jnp.sum(shift * squares, axis=1) + energy[:, 0]], axis=1)
        got = trade(jnp.broadcast_to(own[:, None, :], (width, peers, 2)))
        norm, product = jnp.sum(got, axis=1).T
        return None, norm, product, extended[:, count:]
    summed, energy = edge_pass(extended, head_rows, tail_slots, weights, "scatter", count)
    own = jnp.stack([jnp.sum(squares, axis=1), jnp.sum(shift * squares, axis=1) + energy[:, 0]], axis=1)
    sent = jnp.concatenate(
        [summed[:, count:].reshape(width, peers, cap), jnp.broadcast_to(own[:, None, :], (width, peers, 2))], axis=2
    )
    got = trade(sent)
    returned = got[:, :, :cap].reshape(width, -1)
    norm, product = jnp.sum(got[:, :, cap:], axis=1).T
    local = summed[:, :count] + jnp.dot(returned, picker(halo_rows, count), precision=lax.Precision.HIGHEST)
    return shift * field + local, norm, product, extended[:, count:]


def body(right_side, shift, edge_ends, weights, halo_rows):
    head_rows = edge_ends[0:1]
    tail_slots = edge_ends[1:2]
    weights = weights[None, :]
    share = edge_ends.shape[1] // lax.axis_size("col")
    start = lax.axis_index("col") * share
    quarter = [lax.dynamic_slice_in_dim(item, start, share, axis=1) for item in (head_rows, tail_slots, weights)]
    solution = jnp.zeros_like(right_side)
    residual = right_side
    image, norm_now, product, mirrored = operate(residual, shift, head_rows, tail_slots, weights, halo_rows)
    alpha = norm_now / product
    direction = residual
    along = image
    far_solution = jnp.zeros_like(mirrored)
    far_direction = mirrored
    for step in range(ITERS):
        solution = solution + alpha[:, None] * direction
        far_solution = far_solution + alpha[:, None] * far_direction
        residual = None if along is None else residual - alpha[:, None] * along
        if step + 1 < ITERS:
            image, norm_next, product, mirrored = operate(
                residual, shift, head_rows, tail_slots, weights, halo_rows, step + 2 < ITERS
            )
            ratio = norm_next / norm_now
            alpha = norm_next / (product - ratio * norm_next / alpha)
            direction = residual + ratio[:, None] * direction
            far_direction = mirrored + ratio[:, None] * far_direction
            along = None if image is None else image + ratio[:, None] * along
            norm_now = norm_next
    extended = jnp.concatenate([solution, far_solution], axis=1)
    total = edge_pass(lax.all_gather(extended, "col", axis=0, tiled=True), *quarter, "gap", solution.shape[1])[0]
    resistance = lax.all_gather(total, "col", axis=0, tiled=True)
    return (solution, resistance)


def solution(mesh):
    placed = (
        P("col", ("vx", "vy")),
        P(("vx", "vy")),
        P(None, ("vx", "vy")),
        P(("vx", "vy")),
        P(("vx", "vy"), None),
    )
    return jax.shard_map(
        body,
        mesh=mesh,
        in_specs=placed,
        out_specs=(P("col", ("vx", "vy")), P(("vx", "vy"))),
        check_vma=False,
    )
```

```python
import jax
import jax.numpy as jnp
from jax import lax
from jax.experimental import pallas as pl
from jax.experimental.pallas import tpu as pltpu
from jax.sharding import PartitionSpec as P

ITERS = 2


def trade(blocks):
    return lax.all_to_all(blocks, ("vx", "vy"), split_axis=1, concat_axis=1, tiled=True)


def split3(values):
    first = values.astype(jnp.bfloat16)
    rest = values - first.astype(jnp.float32)
    second = rest.astype(jnp.bfloat16)
    third = (rest - second.astype(jnp.float32)).astype(jnp.bfloat16)
    return jnp.concatenate([first, second, third], axis=0)


def edge_tile(rows):
    return 2048 if rows <= 2048 else 256


def incidence(head, tail, rows, local):
    tile = head.shape[1]
    if rows % 128:
        def build(first, size):
            index = lax.broadcasted_iota(jnp.int32, (size, tile), 0) + first
            ends = (index == head).astype(jnp.float32) - (index == tail).astype(jnp.float32)
            return ends.astype(jnp.bfloat16)

        return build
    lane = lax.broadcasted_iota(jnp.int32, (128, tile), 0)
    low_head = (lane == (head & 127)).astype(jnp.bfloat16)
    low_tail = (lane == (tail & 127)).astype(jnp.bfloat16)
    high_head = head >> 7
    high_tail = tail >> 7

    def build(first, size):
        blocks = []
        for block in range(first // 128, (first + size) // 128):
            off_tail = -(high_tail == block).astype(jnp.bfloat16)
            if block * 128 < local:
                on_head = (high_head == block).astype(jnp.bfloat16)
                blocks.append(low_head * on_head + low_tail * off_tail)
            else:
                blocks.append(low_tail * off_tail)
        return jnp.concatenate(blocks, axis=0) if len(blocks) > 1 else blocks[0]

    return build


def pieces(rows):
    step = 256 if rows % 256 == 0 else (128 if rows % 128 == 0 else rows)
    return [(first, step) for first in range(0, rows, step)]


def flow_kernel(mode, local):
    scatter = mode == "scatter"

    def kernel(xs_ref, head_ref, tail_ref, w_ref, *out_ref):
        out_ref, acc = (out_ref[:2], out_ref[2:]) if scatter else (out_ref[0], ())
        step = pl.program_id(0)
        width, rows = xs_ref.shape
        head = head_ref[...]
        tail = tail_ref[...]
        xs = split3(xs_ref[...])
        parts = []
        gap = None
        build = incidence(head, tail, rows, local)
        for first, size in pieces(rows):
            ends = build(first, size)
            parts.append(ends)
            term = jnp.dot(xs[:, first:first + size], ends, preferred_element_type=jnp.float32)
            gap = term if gap is None else gap + term
        gap = gap[:width] + gap[width:2 * width] + gap[2 * width:]
        if mode == "gap":
            out_ref[...] = jnp.sum(gap * gap, axis=0, keepdims=True)
            return
        weighted = gap * w_ref[...]
        energy = jnp.sum(gap * weighted, axis=1, keepdims=True)
        if mode == "energy":
            out_ref[...] = jnp.where(step == 0, 0.0, out_ref[...]) + energy
            return
        (total,) = acc
        energy_ref = out_ref[1]
        out_ref = out_ref[0]
        energy_ref[...] = jnp.where(step == 0, 0.0, energy_ref[...]) + energy
        flow = split3(weighted)
        dims = (((1,), (1,)), ((), ()))
        for (first, size), ends in zip(pieces(rows), parts):
            window = total[:, first:first + size]
            total[:, first:first + size] = jnp.where(step == 0, 0.0, window) + lax.dot_general(
                flow, ends, dims, preferred_element_type=jnp.float32
            )

        @pl.when(step == pl.num_programs(0) - 1)
        def _():
            sums = total[...]
            out_ref[...] = sums[:width] + sums[width:2 * width] + sums[2 * width:]

    return kernel


def front_kernel(local):
    def kernel(xs_ref, head_ref, tail_ref, w_ref, far_ref, energy_ref, flow_ref, total):
        step = pl.program_id(0)
        width, rows = xs_ref.shape
        xs = split3(xs_ref[...])
        build = incidence(head_ref[...], tail_ref[...], rows, local)
        parts = []
        gap = None
        for first, size in pieces(rows):
            ends = build(first, size)
            parts.append((first, size, ends))
            term = jnp.dot(xs[:, first:first + size], ends, preferred_element_type=jnp.float32)
            gap = term if gap is None else gap + term
        gap = gap[:width] + gap[width:2 * width] + gap[2 * width:]
        weighted = gap * w_ref[...]
        energy = jnp.sum(gap * weighted, axis=1, keepdims=True)
        energy_ref[...] = jnp.where(step == 0, 0.0, energy_ref[...]) + energy
        flow = split3(weighted)
        flow_ref[...] = flow
        dims = (((1,), (1,)), ((), ()))
        for first, size, ends in parts:
            if first < local:
                continue
            window = total[:, first - local:first - local + size]
            total[:, first - local:first - local + size] = jnp.where(step == 0, 0.0, window) + lax.dot_general(
                flow, ends, dims, preferred_element_type=jnp.float32
            )

        @pl.when(step == pl.num_programs(0) - 1)
        def _():
            sums = total[...]
            far_ref[...] = sums[:width] + sums[width:2 * width] + sums[2 * width:]

    return kernel


def back_kernel(rows):
    def kernel(flow_ref, head_ref, tail_ref, near_ref, total):
        step = pl.program_id(0)
        width, local = near_ref.shape
        build = incidence(head_ref[...], tail_ref[...], rows, local)
        flow = flow_ref[...]
        dims = (((1,), (1,)), ((), ()))
        for first, size in pieces(rows):
            if first >= local:
                continue
            ends = build(first, size)
            window = total[:, first:first + size]
            total[:, first:first + size] = jnp.where(step == 0, 0.0, window) + lax.dot_general(
                flow, ends, dims, preferred_element_type=jnp.float32
            )

        @pl.when(step == pl.num_programs(0) - 1)
        def _():
            sums = total[...]
            near_ref[...] = sums[:width] + sums[width:2 * width] + sums[2 * width:]

    return kernel


def split_pass(extended, head_rows, tail_slots, weights, local):
    width, rows = extended.shape
    edges = head_rows.shape[1]
    tile = edge_tile(rows)
    edge_spec = pl.BlockSpec((1, tile), lambda i: (0, i))
    flow_spec = pl.BlockSpec((3 * width, tile), lambda i: (0, i))
    params = pltpu.CompilerParams(dimension_semantics=("arbitrary",), vmem_limit_bytes=48 * 1024 * 1024)
    far, energy, flow = pl.pallas_call(
        front_kernel(local),
        grid=(edges // tile,),
        in_specs=[pl.BlockSpec((width, rows), lambda i: (0, 0)), edge_spec, edge_spec, edge_spec],
        out_specs=(
            pl.BlockSpec((width, rows - local), lambda i: (0, 0)),
            pl.BlockSpec((width, 1), lambda i: (0, 0)),
            flow_spec,
        ),
        out_shape=(
            jax.ShapeDtypeStruct((width, rows - local), jnp.float32),
            jax.ShapeDtypeStruct((width, 1), jnp.float32),
            jax.ShapeDtypeStruct((3 * width, edges), jnp.bfloat16),
        ),
        scratch_shapes=[pltpu.VMEM((3 * width, rows - local), jnp.float32)],
        compiler_params=params,
    )(extended, head_rows, tail_slots, weights)

    def near():
        return pl.pallas_call(
            back_kernel(rows),
            grid=(edges // tile,),
            in_specs=[flow_spec, edge_spec, edge_spec],
            out_specs=pl.BlockSpec((width, local), lambda i: (0, 0)),
            out_shape=jax.ShapeDtypeStruct((width, local), jnp.float32),
            scratch_shapes=[pltpu.VMEM((3 * width, local), jnp.float32)],
            compiler_params=params,
        )(flow, head_rows, tail_slots)

    return far, energy, near


def edge_pass(extended, head_rows, tail_slots, weights, mode, local):
    width, rows = extended.shape
    edges = head_rows.shape[1]
    tile = edge_tile(rows)
    edge_spec = pl.BlockSpec((1, tile), lambda i: (0, i))
    full = pl.BlockSpec((width, rows), lambda i: (0, 0))
    if mode == "scatter":
        out_shape = (jax.ShapeDtypeStruct((width, rows), jnp.float32), jax.ShapeDtypeStruct((width, 1), jnp.float32))
        out_spec = (pl.BlockSpec((width, rows), lambda i: (0, 0)), pl.BlockSpec((width, 1), lambda i: (0, 0)))
        scratch = [pltpu.VMEM((3 * width, rows), jnp.float32)]
    elif mode == "energy":
        out_shape = jax.ShapeDtypeStruct((width, 1), jnp.float32)
        out_spec = pl.BlockSpec((width, 1), lambda i: (0, 0))
        scratch = []
    else:
        out_shape = jax.ShapeDtypeStruct((1, edges), jnp.float32)
        out_spec = edge_spec
        scratch = []
    return pl.pallas_call(
        flow_kernel(mode, local),
        grid=(edges // tile,),
        in_specs=[full, edge_spec, edge_spec, edge_spec],
        out_specs=out_spec,
        out_shape=out_shape,
        scratch_shapes=scratch,
        compiler_params=pltpu.CompilerParams(
            dimension_semantics=("arbitrary",), vmem_limit_bytes=48 * 1024 * 1024
        ),
    )(extended, head_rows, tail_slots, weights)


def picker(halo_rows, count):
    flat = halo_rows.reshape(-1, 1)
    return (flat == lax.broadcasted_iota(jnp.int32, (flat.shape[0], count), 1)).astype(jnp.float32)


def extend(field, halo_rows):
    peers, cap = halo_rows.shape
    chosen = jnp.dot(field, picker(halo_rows, field.shape[1]).T, precision=lax.Precision.HIGHEST)
    mirrored = trade(chosen.reshape(field.shape[0], peers, cap))
    return jnp.concatenate([field, mirrored.reshape(field.shape[0], -1)], axis=1)


def operate(field, shift, head_rows, tail_slots, weights, halo_rows, full=True):
    count = field.shape[1]
    width = field.shape[0]
    peers, cap = halo_rows.shape
    extended = extend(field, halo_rows)
    squares = field * field
    if not full:
        energy = edge_pass(extended, head_rows, tail_slots, weights, "energy", count)
        own = jnp.stack([jnp.sum(squares, axis=1), jnp.sum(shift * squares, axis=1) + energy[:, 0]], axis=1)
        got = trade(jnp.broadcast_to(own[:, None, :], (width, peers, 2)))
        norm, product = jnp.sum(got, axis=1).T
        return None, norm, product, extended[:, count:]
    far, energy, near = split_pass(extended, head_rows, tail_slots, weights, count)
    own = jnp.stack([jnp.sum(squares, axis=1), jnp.sum(shift * squares, axis=1) + energy[:, 0]], axis=1)
    sent = jnp.concatenate(
        [far.reshape(width, peers, cap), jnp.broadcast_to(own[:, None, :], (width, peers, 2))], axis=2
    )
    got = trade(sent)
    returned = got[:, :, :cap].reshape(width, -1)
    norm, product = jnp.sum(got[:, :, cap:], axis=1).T
    local = near() + jnp.dot(returned, picker(halo_rows, count), precision=lax.Precision.HIGHEST)
    return shift * field + local, norm, product, extended[:, count:]


def body(right_side, shift, edge_ends, weights, halo_rows):
    head_rows = edge_ends[0:1]
    tail_slots = edge_ends[1:2]
    weights = weights[None, :]
    share = edge_ends.shape[1] // lax.axis_size("col")
    start = lax.axis_index("col") * share
    quarter = [lax.dynamic_slice_in_dim(item, start, share, axis=1) for item in (head_rows, tail_slots, weights)]
    solution = jnp.zeros_like(right_side)
    residual = right_side
    image, norm_now, product, mirrored = operate(residual, shift, head_rows, tail_slots, weights, halo_rows)
    alpha = norm_now / product
    direction = residual
    along = image
    far_solution = jnp.zeros_like(mirrored)
    far_direction = mirrored
    for step in range(ITERS):
        solution = solution + alpha[:, None] * direction
        far_solution = far_solution + alpha[:, None] * far_direction
        residual = None if along is None else residual - alpha[:, None] * along
        if step + 1 < ITERS:
            image, norm_next, product, mirrored = operate(
                residual, shift, head_rows, tail_slots, weights, halo_rows, step + 2 < ITERS
            )
            ratio = norm_next / norm_now
            alpha = norm_next / (product - ratio * norm_next / alpha)
            direction = residual + ratio[:, None] * direction
            far_direction = mirrored + ratio[:, None] * far_direction
            along = None if image is None else image + ratio[:, None] * along
            norm_now = norm_next
    extended = jnp.concatenate([solution, far_solution], axis=1)
    total = edge_pass(lax.all_gather(extended, "col", axis=0, tiled=True), *quarter, "gap", solution.shape[1])[0]
    resistance = lax.all_gather(total, "col", axis=0, tiled=True)
    return (solution, resistance)


def solution(mesh):
    placed = (
        P("col", ("vx", "vy")),
        P(("vx", "vy")),
        P(None, ("vx", "vy")),
        P(("vx", "vy")),
        P(("vx", "vy"), None),
    )
    return jax.shard_map(
        body,
        mesh=mesh,
        in_specs=placed,
        out_specs=(P("col", ("vx", "vy")), P(("vx", "vy"))),
        check_vma=False,
    )
```

```python
import jax
import jax.numpy as jnp
from jax import lax
from jax.experimental import pallas as pl
from jax.experimental.pallas import tpu as pltpu
from jax.sharding import PartitionSpec as P

ITERS = 2


def trade(blocks):
    return lax.all_to_all(blocks, ("vx", "vy"), split_axis=1, concat_axis=1, tiled=True)


def split3(values):
    first = values.astype(jnp.bfloat16)
    rest = values - first.astype(jnp.float32)
    second = rest.astype(jnp.bfloat16)
    third = (rest - second.astype(jnp.float32)).astype(jnp.bfloat16)
    return jnp.concatenate([first, second, third], axis=0)


def edge_tile(rows):
    return 2048 if rows <= 2048 else 256


def incidence(head, tail, rows, local):
    tile = head.shape[1]
    if rows % 128:
        def build(first, size):
            index = lax.broadcasted_iota(jnp.int32, (size, tile), 0) + first
            ends = (index == head).astype(jnp.float32) - (index == tail).astype(jnp.float32)
            return ends.astype(jnp.bfloat16)

        return build
    lane = lax.broadcasted_iota(jnp.int32, (128, tile), 0).astype(jnp.bfloat16)
    one = jnp.ones((), jnp.bfloat16)
    zero = jnp.zeros((), jnp.bfloat16)
    low_head = jnp.where(lane == (head & 127).astype(jnp.bfloat16), one, zero)
    low_tail = jnp.where(lane == (tail & 127).astype(jnp.bfloat16), one, zero)
    count = -(-rows // 128)
    slots = -(-count // 16) * 16
    which = lax.broadcasted_iota(jnp.int32, (slots, tile), 0)
    on_heads = jnp.where(which == (head >> 7), one, zero)
    off_tails = jnp.where(which == (tail >> 7), -one, zero)

    def build(first, size):
        blocks = []
        for block in range(first // 128, (first + size) // 128):
            off_tail = off_tails[block:block + 1]
            if block * 128 < local:
                blocks.append(low_head * on_heads[block:block + 1] + low_tail * off_tail)
            else:
                blocks.append(low_tail * off_tail)
        return jnp.concatenate(blocks, axis=0) if len(blocks) > 1 else blocks[0]

    return build


def pieces(rows):
    step = 256 if rows % 256 == 0 else (128 if rows % 128 == 0 else rows)
    return [(first, step) for first in range(0, rows, step)]


def flow_kernel(mode, local):
    scatter = mode == "scatter"

    def kernel(xs_ref, head_ref, tail_ref, w_ref, *out_ref):
        out_ref, acc = (out_ref[:2], out_ref[2:]) if scatter else (out_ref[0], ())
        step = pl.program_id(0)
        width, rows = xs_ref.shape
        head = head_ref[...]
        tail = tail_ref[...]
        xs = split3(xs_ref[...])
        parts = []
        gap = None
        build = incidence(head, tail, rows, local)
        for first, size in pieces(rows):
            ends = build(first, size)
            parts.append(ends)
            term = jnp.dot(xs[:, first:first + size], ends, preferred_element_type=jnp.float32)
            gap = term if gap is None else gap + term
        gap = gap[:width] + gap[width:2 * width] + gap[2 * width:]
        if mode == "gap":
            out_ref[...] = jnp.sum(gap * gap, axis=0, keepdims=True)
            return
        weighted = gap * w_ref[...]
        energy = jnp.sum(gap * weighted, axis=1, keepdims=True)
        if mode == "energy":
            out_ref[...] = jnp.where(step == 0, 0.0, out_ref[...]) + energy
            return
        (total,) = acc
        energy_ref = out_ref[1]
        out_ref = out_ref[0]
        energy_ref[...] = jnp.where(step == 0, 0.0, energy_ref[...]) + energy
        flow = split3(weighted)
        dims = (((1,), (1,)), ((), ()))
        for (first, size), ends in zip(pieces(rows), parts):
            window = total[:, first:first + size]
            total[:, first:first + size] = jnp.where(step == 0, 0.0, window) + lax.dot_general(
                flow, ends, dims, preferred_element_type=jnp.float32
            )

        @pl.when(step == pl.num_programs(0) - 1)
        def _():
            sums = total[...]
            out_ref[...] = sums[:width] + sums[width:2 * width] + sums[2 * width:]

    return kernel


def edge_pass(extended, head_rows, tail_slots, weights, mode, local):
    width, rows = extended.shape
    edges = head_rows.shape[1]
    tile = edge_tile(rows)
    edge_spec = pl.BlockSpec((1, tile), lambda i: (0, i))
    full = pl.BlockSpec((width, rows), lambda i: (0, 0))
    if mode == "scatter":
        out_shape = (jax.ShapeDtypeStruct((width, rows), jnp.float32), jax.ShapeDtypeStruct((width, 1), jnp.float32))
        out_spec = (pl.BlockSpec((width, rows), lambda i: (0, 0)), pl.BlockSpec((width, 1), lambda i: (0, 0)))
        scratch = [pltpu.VMEM((3 * width, rows), jnp.float32)]
    elif mode == "energy":
        out_shape = jax.ShapeDtypeStruct((width, 1), jnp.float32)
        out_spec = pl.BlockSpec((width, 1), lambda i: (0, 0))
        scratch = []
    else:
        out_shape = jax.ShapeDtypeStruct((1, edges), jnp.float32)
        out_spec = edge_spec
        scratch = []
    return pl.pallas_call(
        flow_kernel(mode, local),
        grid=(edges // tile,),
        in_specs=[full, edge_spec, edge_spec, edge_spec],
        out_specs=out_spec,
        out_shape=out_shape,
        scratch_shapes=scratch,
        compiler_params=pltpu.CompilerParams(
            dimension_semantics=("arbitrary",), vmem_limit_bytes=48 * 1024 * 1024
        ),
    )(extended, head_rows, tail_slots, weights)


def picker(halo_rows, count):
    flat = halo_rows.reshape(-1, 1)
    return (flat == lax.broadcasted_iota(jnp.int32, (flat.shape[0], count), 1)).astype(jnp.float32)


def extend(field, halo_rows):
    peers, cap = halo_rows.shape
    chosen = jnp.dot(field, picker(halo_rows, field.shape[1]).T, precision=lax.Precision.HIGHEST)
    mirrored = trade(chosen.reshape(field.shape[0], peers, cap))
    return jnp.concatenate([field, mirrored.reshape(field.shape[0], -1)], axis=1)


def operate(field, shift, head_rows, tail_slots, weights, halo_rows, full=True):
    count = field.shape[1]
    width = field.shape[0]
    peers, cap = halo_rows.shape
    extended = extend(field, halo_rows)
    squares = field * field
    if not full:
        energy = edge_pass(extended, head_rows, tail_slots, weights, "energy", count)
        own = jnp.stack([jnp.sum(squares, axis=1), jnp.sum(shift * squares, axis=1) + energy[:, 0]], axis=1)
        got = trade(jnp.broadcast_to(own[:, None, :], (width, peers, 2)))
        norm, product = jnp.sum(got, axis=1).T
        return None, norm, product, extended[:, count:]
    summed, energy = edge_pass(extended, head_rows, tail_slots, weights, "scatter", count)
    own = jnp.stack([jnp.sum(squares, axis=1), jnp.sum(shift * squares, axis=1) + energy[:, 0]], axis=1)
    sent = jnp.concatenate(
        [summed[:, count:].reshape(width, peers, cap), jnp.broadcast_to(own[:, None, :], (width, peers, 2))], axis=2
    )
    got = trade(sent)
    returned = got[:, :, :cap].reshape(width, -1)
    norm, product = jnp.sum(got[:, :, cap:], axis=1).T
    local = summed[:, :count] + jnp.dot(returned, picker(halo_rows, count), precision=lax.Precision.HIGHEST)
    return shift * field + local, norm, product, extended[:, count:]


def body(right_side, shift, edge_ends, weights, halo_rows):
    head_rows = edge_ends[0:1]
    tail_slots = edge_ends[1:2]
    weights = weights[None, :]
    share = edge_ends.shape[1] // lax.axis_size("col")
    start = lax.axis_index("col") * share
    quarter = [lax.dynamic_slice_in_dim(item, start, share, axis=1) for item in (head_rows, tail_slots, weights)]
    solution = jnp.zeros_like(right_side)
    residual = right_side
    image, norm_now, product, mirrored = operate(residual, shift, head_rows, tail_slots, weights, halo_rows)
    alpha = norm_now / product
    direction = residual
    along = image
    far_solution = jnp.zeros_like(mirrored)
    far_direction = mirrored
    for step in range(ITERS):
        solution = solution + alpha[:, None] * direction
        far_solution = far_solution + alpha[:, None] * far_direction
        residual = None if along is None else residual - alpha[:, None] * along
        if step + 1 < ITERS:
            image, norm_next, product, mirrored = operate(
                residual, shift, head_rows, tail_slots, weights, halo_rows, step + 2 < ITERS
            )
            ratio = norm_next / norm_now
            alpha = norm_next / (product - ratio * norm_next / alpha)
            direction = residual + ratio[:, None] * direction
            far_direction = mirrored + ratio[:, None] * far_direction
            along = None if image is None else image + ratio[:, None] * along
            norm_now = norm_next
    extended = jnp.concatenate([solution, far_solution], axis=1)
    total = edge_pass(lax.all_gather(extended, "col", axis=0, tiled=True), *quarter, "gap", solution.shape[1])[0]
    resistance = lax.all_gather(total, "col", axis=0, tiled=True)
    return (solution, resistance)


def solution(mesh):
    placed = (
        P("col", ("vx", "vy")),
        P(("vx", "vy")),
        P(None, ("vx", "vy")),
        P(("vx", "vy")),
        P(("vx", "vy"), None),
    )
    return jax.shard_map(
        body,
        mesh=mesh,
        in_specs=placed,
        out_specs=(P("col", ("vx", "vy")), P(("vx", "vy"))),
        check_vma=False,
    )
```

```python
import jax
import jax.numpy as jnp
from jax import lax
from jax.experimental import pallas as pl
from jax.experimental.pallas import tpu as pltpu
from jax.sharding import PartitionSpec as P

ITERS = 2


def trade(blocks):
    return lax.all_to_all(blocks, ("vx", "vy"), split_axis=1, concat_axis=1, tiled=True)


def split3(values):
    first = values.astype(jnp.bfloat16)
    rest = values - first.astype(jnp.float32)
    second = rest.astype(jnp.bfloat16)
    third = (rest - second.astype(jnp.float32)).astype(jnp.bfloat16)
    return jnp.concatenate([first, second, third], axis=0)


def edge_tile(rows):
    return 2048 if rows <= 2048 else 256


def incidence(head, tail, rows, local):
    tile = head.shape[1]
    if rows % 128:
        def build(first, size):
            index = lax.broadcasted_iota(jnp.int32, (size, tile), 0) + first
            ends = (index == head).astype(jnp.float32) - (index == tail).astype(jnp.float32)
            return ends.astype(jnp.bfloat16)

        return build
    lane = lax.broadcasted_iota(jnp.int32, (128, tile), 0).astype(jnp.bfloat16)
    one = jnp.ones((), jnp.bfloat16)
    zero = jnp.zeros((), jnp.bfloat16)
    low_head = jnp.where(lane == (head & 127).astype(jnp.bfloat16), one, zero)
    low_tail = jnp.where(lane == (tail & 127).astype(jnp.bfloat16), one, zero)
    count = -(-rows // 128)
    slots = -(-count // 16) * 16
    which = lax.broadcasted_iota(jnp.int32, (slots, tile), 0)
    on_heads = jnp.where(which == (head >> 7), one, zero)
    off_tails = jnp.where(which == (tail >> 7), -one, zero)

    def build(first, size):
        blocks = []
        for block in range(first // 128, (first + size) // 128):
            off_tail = off_tails[block:block + 1]
            if block * 128 < local:
                blocks.append(low_head * on_heads[block:block + 1] + low_tail * off_tail)
            else:
                blocks.append(low_tail * off_tail)
        return jnp.concatenate(blocks, axis=0) if len(blocks) > 1 else blocks[0]

    return build


def pieces(rows):
    step = 256 if rows % 256 == 0 else (128 if rows % 128 == 0 else rows)
    return [(first, step) for first in range(0, rows, step)]


def flow_kernel(mode, local):
    scatter = mode == "scatter"

    def kernel(xs_ref, head_ref, tail_ref, w_ref, *out_ref):
        out_ref, acc = (out_ref[:2], out_ref[2:]) if scatter else (out_ref[0], ())
        step = pl.program_id(0)
        width, rows = xs_ref.shape
        head = head_ref[...]
        tail = tail_ref[...]
        xs = split3(xs_ref[...])
        parts = []
        gap = None
        build = incidence(head, tail, rows, local)
        for first, size in pieces(rows):
            ends = build(first, size)
            parts.append(ends)
            term = jnp.dot(xs[:, first:first + size], ends, preferred_element_type=jnp.float32)
            gap = term if gap is None else gap + term
        gap = gap[:width] + gap[width:2 * width] + gap[2 * width:]
        if mode == "gap":
            out_ref[...] = jnp.sum(gap * gap, axis=0, keepdims=True)
            return
        weighted = gap * w_ref[...]
        energy = jnp.sum(gap * weighted, axis=1, keepdims=True)
        if mode == "energy":
            out_ref[...] = jnp.where(step == 0, 0.0, out_ref[...]) + energy
            return
        (total,) = acc
        energy_ref = out_ref[1]
        out_ref = out_ref[0]
        energy_ref[...] = jnp.where(step == 0, 0.0, energy_ref[...]) + energy
        flow = split3(weighted)
        dims = (((1,), (1,)), ((), ()))
        for (first, size), ends in zip(pieces(rows), parts):
            window = total[:, first:first + size]
            total[:, first:first + size] = jnp.where(step == 0, 0.0, window) + lax.dot_general(
                flow, ends, dims, preferred_element_type=jnp.float32
            )

        @pl.when(step == pl.num_programs(0) - 1)
        def _():
            sums = total[...]
            out_ref[...] = sums[:width] + sums[width:2 * width] + sums[2 * width:]

    return kernel


def edge_pass(extended, head_rows, tail_slots, weights, mode, local):
    width, rows = extended.shape
    edges = head_rows.shape[1]
    tile = edge_tile(rows)
    edge_spec = pl.BlockSpec((1, tile), lambda i: (0, i))
    full = pl.BlockSpec((width, rows), lambda i: (0, 0))
    if mode == "scatter":
        out_shape = (jax.ShapeDtypeStruct((width, rows), jnp.float32), jax.ShapeDtypeStruct((width, 1), jnp.float32))
        out_spec = (pl.BlockSpec((width, rows), lambda i: (0, 0)), pl.BlockSpec((width, 1), lambda i: (0, 0)))
        scratch = [pltpu.VMEM((3 * width, rows), jnp.float32)]
    elif mode == "energy":
        out_shape = jax.ShapeDtypeStruct((width, 1), jnp.float32)
        out_spec = pl.BlockSpec((width, 1), lambda i: (0, 0))
        scratch = []
    else:
        out_shape = jax.ShapeDtypeStruct((1, edges), jnp.float32)
        out_spec = edge_spec
        scratch = []
    return pl.pallas_call(
        flow_kernel(mode, local),
        grid=(edges // tile,),
        in_specs=[full, edge_spec, edge_spec, edge_spec],
        out_specs=out_spec,
        out_shape=out_shape,
        scratch_shapes=scratch,
        compiler_params=pltpu.CompilerParams(
            dimension_semantics=("arbitrary",), vmem_limit_bytes=48 * 1024 * 1024
        ),
    )(extended, head_rows, tail_slots, weights)


def picker(halo_rows, count):
    peers, cap = halo_rows.shape
    index = lax.broadcasted_iota(jnp.int32, (peers, cap, count), 2)
    return (halo_rows[:, :, None] == index).astype(jnp.float32)


def extend(field, halo_rows):
    chosen = jnp.einsum("cv,psv->cps", field, picker(halo_rows, field.shape[1]), precision=lax.Precision.HIGHEST)
    mirrored = trade(chosen)
    return jnp.concatenate([field, mirrored.reshape(field.shape[0], -1)], axis=1)


def operate(field, shift, head_rows, tail_slots, weights, halo_rows, full=True):
    count = field.shape[1]
    width = field.shape[0]
    peers, cap = halo_rows.shape
    extended = extend(field, halo_rows)
    squares = field * field
    if not full:
        energy = edge_pass(extended, head_rows, tail_slots, weights, "energy", count)
        own = jnp.stack([jnp.sum(squares, axis=1), jnp.sum(shift * squares, axis=1) + energy[:, 0]], axis=1)
        got = trade(jnp.broadcast_to(own[:, None, :], (width, peers, 2)))
        norm, product = jnp.sum(got, axis=1).T
        return None, norm, product, extended[:, count:]
    summed, energy = edge_pass(extended, head_rows, tail_slots, weights, "scatter", count)
    own = jnp.stack([jnp.sum(squares, axis=1), jnp.sum(shift * squares, axis=1) + energy[:, 0]], axis=1)
    sent = jnp.concatenate(
        [summed[:, count:].reshape(width, peers, cap), jnp.broadcast_to(own[:, None, :], (width, peers, 2))], axis=2
    )
    got = trade(sent)
    returned = got[:, :, :cap]
    norm, product = jnp.sum(got[:, :, cap:], axis=1).T
    local = summed[:, :count] + jnp.einsum(
        "cps,psv->cv", returned, picker(halo_rows, count), precision=lax.Precision.HIGHEST
    )
    return shift * field + local, norm, product, extended[:, count:]


def body(right_side, shift, edge_ends, weights, halo_rows):
    head_rows = edge_ends[0:1]
    tail_slots = edge_ends[1:2]
    weights = weights[None, :]
    share = edge_ends.shape[1] // lax.axis_size("col")
    start = lax.axis_index("col") * share
    quarter = [lax.dynamic_slice_in_dim(item, start, share, axis=1) for item in (head_rows, tail_slots, weights)]
    solution = jnp.zeros_like(right_side)
    residual = right_side
    image, norm_now, product, mirrored = operate(residual, shift, head_rows, tail_slots, weights, halo_rows)
    alpha = norm_now / product
    direction = residual
    along = image
    far_solution = jnp.zeros_like(mirrored)
    far_direction = mirrored
    for step in range(ITERS):
        solution = solution + alpha[:, None] * direction
        far_solution = far_solution + alpha[:, None] * far_direction
        residual = None if along is None else residual - alpha[:, None] * along
        if step + 1 < ITERS:
            image, norm_next, product, mirrored = operate(
                residual, shift, head_rows, tail_slots, weights, halo_rows, step + 2 < ITERS
            )
            ratio = norm_next / norm_now
            alpha = norm_next / (product - ratio * norm_next / alpha)
            direction = residual + ratio[:, None] * direction
            far_direction = mirrored + ratio[:, None] * far_direction
            along = None if image is None else image + ratio[:, None] * along
            norm_now = norm_next
    extended = jnp.concatenate([solution, far_solution], axis=1)
    total = edge_pass(lax.all_gather(extended, "col", axis=0, tiled=True), *quarter, "gap", solution.shape[1])[0]
    resistance = lax.all_gather(total, "col", axis=0, tiled=True)
    return (solution, resistance)


def solution(mesh):
    placed = (
        P("col", ("vx", "vy")),
        P(("vx", "vy")),
        P(None, ("vx", "vy")),
        P(("vx", "vy")),
        P(("vx", "vy"), None),
    )
    return jax.shard_map(
        body,
        mesh=mesh,
        in_specs=placed,
        out_specs=(P("col", ("vx", "vy")), P(("vx", "vy"))),
        check_vma=False,
    )
```

```python
import jax
import jax.numpy as jnp
from jax import lax
from jax.experimental import pallas as pl
from jax.experimental.pallas import tpu as pltpu
from jax.sharding import PartitionSpec as P

ITERS = 2


def trade(blocks):
    return lax.all_to_all(blocks, ("vx", "vy"), split_axis=1, concat_axis=1, tiled=True)


def split3(values):
    first = values.astype(jnp.bfloat16)
    rest = values - first.astype(jnp.float32)
    second = rest.astype(jnp.bfloat16)
    third = (rest - second.astype(jnp.float32)).astype(jnp.bfloat16)
    return jnp.concatenate([first, second, third], axis=0)


def edge_tile(rows):
    return 2048 if rows <= 2048 else 256


def incidence(head, tail, rows, local):
    tile = head.shape[1]
    if rows % 128:
        def build(first, size):
            index = lax.broadcasted_iota(jnp.int32, (size, tile), 0) + first
            ends = (index == head).astype(jnp.float32) - (index == tail).astype(jnp.float32)
            return ends.astype(jnp.bfloat16)

        return build
    lane = lax.broadcasted_iota(jnp.int32, (128, tile), 0).astype(jnp.bfloat16)
    one = jnp.ones((), jnp.bfloat16)
    zero = jnp.zeros((), jnp.bfloat16)
    low_head = jnp.where(lane == (head & 127).astype(jnp.bfloat16), one, zero)
    low_tail = jnp.where(lane == (tail & 127).astype(jnp.bfloat16), one, zero)
    count = -(-rows // 128)
    slots = -(-count // 16) * 16
    which = lax.broadcasted_iota(jnp.int32, (slots, tile), 0)
    on_heads = jnp.where(which == (head >> 7), one, zero)
    off_tails = jnp.where(which == (tail >> 7), -one, zero)

    def build(first, size):
        blocks = []
        for block in range(first // 128, (first + size) // 128):
            off_tail = off_tails[block:block + 1]
            if block * 128 < local:
                blocks.append(low_head * on_heads[block:block + 1] + low_tail * off_tail)
            else:
                blocks.append(low_tail * off_tail)
        return jnp.concatenate(blocks, axis=0) if len(blocks) > 1 else blocks[0]

    return build


def pieces(rows):
    step = 256 if rows % 256 == 0 else (128 if rows % 128 == 0 else rows)
    return [(first, step) for first in range(0, rows, step)]


def flow_kernel(mode, local):
    scatter = mode == "scatter"

    def kernel(xs_ref, head_ref, tail_ref, w_ref, *out_ref):
        out_ref, acc = (out_ref[:2], out_ref[2:]) if scatter else (out_ref[0], ())
        step = pl.program_id(0)
        width, rows = xs_ref.shape
        head = head_ref[...]
        tail = tail_ref[...]
        xs = split3(xs_ref[...])
        parts = []
        gap = None
        build = incidence(head, tail, rows, local)
        for first, size in pieces(rows):
            ends = build(first, size)
            parts.append(ends)
            term = jnp.dot(xs[:, first:first + size], ends, preferred_element_type=jnp.float32)
            gap = term if gap is None else gap + term
        gap = gap[:width] + gap[width:2 * width] + gap[2 * width:]
        if mode == "gap":
            out_ref[...] = jnp.sum(gap * gap, axis=0, keepdims=True)
            return
        weighted = gap * w_ref[...]
        energy = jnp.sum(gap * weighted, axis=1, keepdims=True)
        if mode == "energy":
            out_ref[...] = jnp.where(step == 0, 0.0, out_ref[...]) + energy
            return
        (total,) = acc
        energy_ref = out_ref[1]
        out_ref = out_ref[0]
        energy_ref[...] = jnp.where(step == 0, 0.0, energy_ref[...]) + energy
        flow = split3(weighted)
        dims = (((1,), (1,)), ((), ()))
        for (first, size), ends in zip(pieces(rows), parts):
            window = total[:, first:first + size]
            total[:, first:first + size] = jnp.where(step == 0, 0.0, window) + lax.dot_general(
                flow, ends, dims, preferred_element_type=jnp.float32
            )

        @pl.when(step == pl.num_programs(0) - 1)
        def _():
            sums = total[...]
            out_ref[...] = sums[:width] + sums[width:2 * width] + sums[2 * width:]

    return kernel


def edge_pass(extended, head_rows, tail_slots, weights, mode, local):
    width, rows = extended.shape
    edges = head_rows.shape[1]
    tile = edge_tile(rows)
    edge_spec = pl.BlockSpec((1, tile), lambda i: (0, i))
    full = pl.BlockSpec((width, rows), lambda i: (0, 0))
    if mode == "scatter":
        out_shape = (jax.ShapeDtypeStruct((width, rows), jnp.float32), jax.ShapeDtypeStruct((width, 1), jnp.float32))
        out_spec = (pl.BlockSpec((width, rows), lambda i: (0, 0)), pl.BlockSpec((width, 1), lambda i: (0, 0)))
        scratch = [pltpu.VMEM((3 * width, rows), jnp.float32)]
    elif mode == "energy":
        out_shape = jax.ShapeDtypeStruct((width, 1), jnp.float32)
        out_spec = pl.BlockSpec((width, 1), lambda i: (0, 0))
        scratch = []
    else:
        out_shape = jax.ShapeDtypeStruct((1, edges), jnp.float32)
        out_spec = edge_spec
        scratch = []
    return pl.pallas_call(
        flow_kernel(mode, local),
        grid=(edges // tile,),
        in_specs=[full, edge_spec, edge_spec, edge_spec],
        out_specs=out_spec,
        out_shape=out_shape,
        scratch_shapes=scratch,
        compiler_params=pltpu.CompilerParams(
            dimension_semantics=("arbitrary",), vmem_limit_bytes=48 * 1024 * 1024
        ),
    )(extended, head_rows, tail_slots, weights)


def picker(halo_rows, count):
    peers, cap = halo_rows.shape
    index = lax.broadcasted_iota(jnp.int32, (peers, cap, count), 2)
    return (halo_rows[:, :, None] == index).astype(jnp.bfloat16)


def parts3(values):
    first = lax.reduce_precision(values, exponent_bits=8, mantissa_bits=7)
    rest = values - first
    second = lax.reduce_precision(rest, exponent_bits=8, mantissa_bits=7)
    third = rest - second
    return jnp.concatenate([first, second, third], axis=0).astype(jnp.bfloat16)


def pick(pattern, values, choice):
    width = values.shape[0]
    out = jnp.einsum(pattern, parts3(values), choice, preferred_element_type=jnp.float32)
    return out[:width] + out[width:2 * width] + out[2 * width:]


def extend(field, halo_rows):
    chosen = pick("cv,psv->cps", field, picker(halo_rows, field.shape[1]))
    mirrored = trade(chosen)
    return jnp.concatenate([field, mirrored.reshape(field.shape[0], -1)], axis=1)


def operate(field, shift, head_rows, tail_slots, weights, halo_rows, full=True):
    count = field.shape[1]
    width = field.shape[0]
    peers, cap = halo_rows.shape
    extended = extend(field, halo_rows)
    squares = field * field
    if not full:
        energy = edge_pass(extended, head_rows, tail_slots, weights, "energy", count)
        own = jnp.stack([jnp.sum(squares, axis=1), jnp.sum(shift * squares, axis=1) + energy[:, 0]], axis=1)
        got = trade(jnp.broadcast_to(own[:, None, :], (width, peers, 2)))
        norm, product = jnp.sum(got, axis=1).T
        return None, norm, product, extended[:, count:]
    summed, energy = edge_pass(extended, head_rows, tail_slots, weights, "scatter", count)
    own = jnp.stack([jnp.sum(squares, axis=1), jnp.sum(shift * squares, axis=1) + energy[:, 0]], axis=1)
    sent = jnp.concatenate(
        [summed[:, count:].reshape(width, peers, cap), jnp.broadcast_to(own[:, None, :], (width, peers, 2))], axis=2
    )
    got = trade(sent)
    returned = got[:, :, :cap]
    norm, product = jnp.sum(got[:, :, cap:], axis=1).T
    local = summed[:, :count] + pick("cps,psv->cv", returned, picker(halo_rows, count))
    return shift * field + local, norm, product, extended[:, count:]


def body(right_side, shift, edge_ends, weights, halo_rows):
    head_rows = edge_ends[0:1]
    tail_slots = edge_ends[1:2]
    weights = weights[None, :]
    share = edge_ends.shape[1] // lax.axis_size("col")
    start = lax.axis_index("col") * share
    quarter = [lax.dynamic_slice_in_dim(item, start, share, axis=1) for item in (head_rows, tail_slots, weights)]
    solution = jnp.zeros_like(right_side)
    residual = right_side
    image, norm_now, product, mirrored = operate(residual, shift, head_rows, tail_slots, weights, halo_rows)
    alpha = norm_now / product
    direction = residual
    along = image
    far_solution = jnp.zeros_like(mirrored)
    far_direction = mirrored
    for step in range(ITERS):
        solution = solution + alpha[:, None] * direction
        far_solution = far_solution + alpha[:, None] * far_direction
        residual = None if along is None else residual - alpha[:, None] * along
        if step + 1 < ITERS:
            image, norm_next, product, mirrored = operate(
                residual, shift, head_rows, tail_slots, weights, halo_rows, step + 2 < ITERS
            )
            ratio = norm_next / norm_now
            alpha = norm_next / (product - ratio * norm_next / alpha)
            direction = residual + ratio[:, None] * direction
            far_direction = mirrored + ratio[:, None] * far_direction
            along = None if image is None else image + ratio[:, None] * along
            norm_now = norm_next
    extended = jnp.concatenate([solution, far_solution], axis=1)
    total = edge_pass(lax.all_gather(extended, "col", axis=0, tiled=True), *quarter, "gap", solution.shape[1])[0]
    resistance = lax.all_gather(total, "col", axis=0, tiled=True)
    return (solution, resistance)


def solution(mesh):
    placed = (
        P("col", ("vx", "vy")),
        P(("vx", "vy")),
        P(None, ("vx", "vy")),
        P(("vx", "vy")),
        P(("vx", "vy"), None),
    )
    return jax.shard_map(
        body,
        mesh=mesh,
        in_specs=placed,
        out_specs=(P("col", ("vx", "vy")), P(("vx", "vy"))),
        check_vma=False,
    )
```

```python
import jax
import jax.numpy as jnp
from jax import lax
from jax.experimental import pallas as pl
from jax.experimental.pallas import tpu as pltpu
from jax.sharding import PartitionSpec as P

ITERS = 2


def trade(blocks):
    return lax.all_to_all(blocks, ("vx", "vy"), split_axis=1, concat_axis=1, tiled=True)


def split3(values):
    first = values.astype(jnp.bfloat16)
    rest = values - first.astype(jnp.float32)
    second = rest.astype(jnp.bfloat16)
    third = (rest - second.astype(jnp.float32)).astype(jnp.bfloat16)
    return jnp.concatenate([first, second, third], axis=0)


def edge_tile(rows):
    return 2048 if rows <= 2048 else 256


def incidence(head, tail, rows, local):
    tile = head.shape[1]
    if rows % 128:
        def build(first, size):
            index = lax.broadcasted_iota(jnp.int32, (size, tile), 0) + first
            ends = (index == head).astype(jnp.float32) - (index == tail).astype(jnp.float32)
            return ends.astype(jnp.bfloat16)

        return build
    lane = lax.broadcasted_iota(jnp.int32, (128, tile), 0).astype(jnp.bfloat16)
    one = jnp.ones((), jnp.bfloat16)
    zero = jnp.zeros((), jnp.bfloat16)
    low_head = jnp.where(lane == (head & 127).astype(jnp.bfloat16), one, zero)
    low_tail = jnp.where(lane == (tail & 127).astype(jnp.bfloat16), one, zero)
    count = -(-rows // 128)
    slots = -(-count // 16) * 16
    which = lax.broadcasted_iota(jnp.int32, (slots, tile), 0)
    on_heads = jnp.where(which == (head >> 7), one, zero)
    off_tails = jnp.where(which == (tail >> 7), -one, zero)

    def build(first, size):
        blocks = []
        for block in range(first // 128, (first + size) // 128):
            off_tail = off_tails[block:block + 1]
            if block * 128 < local:
                blocks.append(low_head * on_heads[block:block + 1] + low_tail * off_tail)
            else:
                blocks.append(low_tail * off_tail)
        return jnp.concatenate(blocks, axis=0) if len(blocks) > 1 else blocks[0]

    return build


def pieces(rows):
    step = 256 if rows % 256 == 0 else (128 if rows % 128 == 0 else rows)
    return [(first, step) for first in range(0, rows, step)]


def flow_kernel(mode, local):
    scatter = mode == "scatter"

    def kernel(xs_ref, head_ref, tail_ref, w_ref, *out_ref):
        out_ref, acc = (out_ref[:2], out_ref[2:]) if scatter else (out_ref[0], ())
        step = pl.program_id(0)
        width, rows = xs_ref.shape
        head = head_ref[...]
        tail = tail_ref[...]
        xs = split3(xs_ref[...])
        parts = []
        gap = None
        build = incidence(head, tail, rows, local)
        for first, size in pieces(rows):
            ends = build(first, size)
            parts.append(ends)
            term = jnp.dot(xs[:, first:first + size], ends, preferred_element_type=jnp.float32)
            gap = term if gap is None else gap + term
        gap = gap[:width] + gap[width:2 * width] + gap[2 * width:]
        if mode == "gap":
            out_ref[...] = jnp.sum(gap * gap, axis=0, keepdims=True)
            return
        weighted = gap * w_ref[...]
        energy = jnp.sum(gap * weighted, axis=1, keepdims=True)
        if mode == "energy":
            out_ref[...] = jnp.where(step == 0, 0.0, out_ref[...]) + energy
            return
        (total,) = acc
        energy_ref = out_ref[1]
        out_ref = out_ref[0]
        energy_ref[...] = jnp.where(step == 0, 0.0, energy_ref[...]) + energy
        flow = split3(weighted)
        dims = (((1,), (1,)), ((), ()))
        for (first, size), ends in zip(pieces(rows), parts):
            window = total[:, first:first + size]
            total[:, first:first + size] = jnp.where(step == 0, 0.0, window) + lax.dot_general(
                flow, ends, dims, preferred_element_type=jnp.float32
            )

        @pl.when(step == pl.num_programs(0) - 1)
        def _():
            sums = total[...]
            out_ref[...] = sums[:width] + sums[width:2 * width] + sums[2 * width:]

    return kernel


def edge_pass(extended, head_rows, tail_slots, weights, mode, local):
    width, rows = extended.shape
    edges = head_rows.shape[1]
    tile = edge_tile(rows)
    if mode == "gap" and rows <= 2048 and edges % 4096 == 0:
        tile = 4096
    edge_spec = pl.BlockSpec((1, tile), lambda i: (0, i))
    full = pl.BlockSpec((width, rows), lambda i: (0, 0))
    if mode == "scatter":
        out_shape = (jax.ShapeDtypeStruct((width, rows), jnp.float32), jax.ShapeDtypeStruct((width, 1), jnp.float32))
        out_spec = (pl.BlockSpec((width, rows), lambda i: (0, 0)), pl.BlockSpec((width, 1), lambda i: (0, 0)))
        scratch = [pltpu.VMEM((3 * width, rows), jnp.float32)]
    elif mode == "energy":
        out_shape = jax.ShapeDtypeStruct((width, 1), jnp.float32)
        out_spec = pl.BlockSpec((width, 1), lambda i: (0, 0))
        scratch = []
    else:
        out_shape = jax.ShapeDtypeStruct((1, edges), jnp.float32)
        out_spec = edge_spec
        scratch = []
    return pl.pallas_call(
        flow_kernel(mode, local),
        grid=(edges // tile,),
        in_specs=[full, edge_spec, edge_spec, edge_spec],
        out_specs=out_spec,
        out_shape=out_shape,
        scratch_shapes=scratch,
        compiler_params=pltpu.CompilerParams(
            dimension_semantics=("arbitrary",), vmem_limit_bytes=48 * 1024 * 1024
        ),
    )(extended, head_rows, tail_slots, weights)


def picker(halo_rows, count):
    peers, cap = halo_rows.shape
    index = lax.broadcasted_iota(jnp.int32, (peers, cap, count), 2)
    return (halo_rows[:, :, None] == index).astype(jnp.bfloat16)


def parts3(values):
    first = lax.reduce_precision(values, exponent_bits=8, mantissa_bits=7)
    rest = values - first
    second = lax.reduce_precision(rest, exponent_bits=8, mantissa_bits=7)
    third = rest - second
    return jnp.concatenate([first, second, third], axis=0).astype(jnp.bfloat16)


def pick(pattern, values, choice):
    width = values.shape[0]
    out = jnp.einsum(pattern, parts3(values), choice, preferred_element_type=jnp.float32)
    return out[:width] + out[width:2 * width] + out[2 * width:]


def extend(field, halo_rows):
    chosen = pick("cv,psv->cps", field, picker(halo_rows, field.shape[1]))
    mirrored = trade(chosen)
    return jnp.concatenate([field, mirrored.reshape(field.shape[0], -1)], axis=1)


def operate(field, shift, head_rows, tail_slots, weights, halo_rows, full=True):
    count = field.shape[1]
    width = field.shape[0]
    peers, cap = halo_rows.shape
    extended = extend(field, halo_rows)
    squares = field * field
    if not full:
        energy = edge_pass(extended, head_rows, tail_slots, weights, "energy", count)
        own = jnp.stack([jnp.sum(squares, axis=1), jnp.sum(shift * squares, axis=1) + energy[:, 0]], axis=1)
        got = trade(jnp.broadcast_to(own[:, None, :], (width, peers, 2)))
        norm, product = jnp.sum(got, axis=1).T
        return None, norm, product, extended[:, count:]
    summed, energy = edge_pass(extended, head_rows, tail_slots, weights, "scatter", count)
    own = jnp.stack([jnp.sum(squares, axis=1), jnp.sum(shift * squares, axis=1) + energy[:, 0]], axis=1)
    sent = jnp.concatenate(
        [summed[:, count:].reshape(width, peers, cap), jnp.broadcast_to(own[:, None, :], (width, peers, 2))], axis=2
    )
    got = trade(sent)
    returned = got[:, :, :cap]
    norm, product = jnp.sum(got[:, :, cap:], axis=1).T
    local = summed[:, :count] + pick("cps,psv->cv", returned, picker(halo_rows, count))
    return shift * field + local, norm, product, extended[:, count:]


def body(right_side, shift, edge_ends, weights, halo_rows):
    head_rows = edge_ends[0:1]
    tail_slots = edge_ends[1:2]
    weights = weights[None, :]
    share = edge_ends.shape[1] // lax.axis_size("col")
    start = lax.axis_index("col") * share
    quarter = [lax.dynamic_slice_in_dim(item, start, share, axis=1) for item in (head_rows, tail_slots, weights)]
    solution = jnp.zeros_like(right_side)
    residual = right_side
    image, norm_now, product, mirrored = operate(residual, shift, head_rows, tail_slots, weights, halo_rows)
    alpha = norm_now / product
    direction = residual
    along = image
    far_solution = jnp.zeros_like(mirrored)
    far_direction = mirrored
    for step in range(ITERS):
        solution = solution + alpha[:, None] * direction
        far_solution = far_solution + alpha[:, None] * far_direction
        residual = None if along is None else residual - alpha[:, None] * along
        if step + 1 < ITERS:
            image, norm_next, product, mirrored = operate(
                residual, shift, head_rows, tail_slots, weights, halo_rows, step + 2 < ITERS
            )
            ratio = norm_next / norm_now
            alpha = norm_next / (product - ratio * norm_next / alpha)
            direction = residual + ratio[:, None] * direction
            far_direction = mirrored + ratio[:, None] * far_direction
            along = None if image is None else image + ratio[:, None] * along
            norm_now = norm_next
    extended = jnp.concatenate([solution, far_solution], axis=1)
    total = edge_pass(lax.all_gather(extended, "col", axis=0, tiled=True), *quarter, "gap", solution.shape[1])[0]
    resistance = lax.all_gather(total, "col", axis=0, tiled=True)
    return (solution, resistance)


def solution(mesh):
    placed = (
        P("col", ("vx", "vy")),
        P(("vx", "vy")),
        P(None, ("vx", "vy")),
        P(("vx", "vy")),
        P(("vx", "vy"), None),
    )
    return jax.shard_map(
        body,
        mesh=mesh,
        in_specs=placed,
        out_specs=(P("col", ("vx", "vy")), P(("vx", "vy"))),
        check_vma=False,
    )
```

```python
import jax
import jax.numpy as jnp
from jax import lax
from jax.experimental import pallas as pl
from jax.experimental.pallas import tpu as pltpu
from jax.sharding import PartitionSpec as P

ITERS = 2


def trade(blocks):
    return lax.all_to_all(blocks, ("vx", "vy"), split_axis=1, concat_axis=1, tiled=True)


def split3(values):
    first = values.astype(jnp.bfloat16)
    rest = values - first.astype(jnp.float32)
    second = rest.astype(jnp.bfloat16)
    third = (rest - second.astype(jnp.float32)).astype(jnp.bfloat16)
    return jnp.concatenate([first, second, third], axis=0)


def edge_tile(rows):
    return 2048 if rows <= 2048 else 256


def incidence(head, tail, rows, local):
    tile = head.shape[1]
    if rows % 128:
        def build(first, size):
            index = lax.broadcasted_iota(jnp.int32, (size, tile), 0) + first
            ends = (index == head).astype(jnp.float32) - (index == tail).astype(jnp.float32)
            return ends.astype(jnp.bfloat16)

        return build
    lane = lax.broadcasted_iota(jnp.int32, (128, tile), 0).astype(jnp.bfloat16)
    one = jnp.ones((), jnp.bfloat16)
    zero = jnp.zeros((), jnp.bfloat16)
    low_head = jnp.where(lane == (head & 127).astype(jnp.bfloat16), one, zero)
    low_tail = jnp.where(lane == (tail & 127).astype(jnp.bfloat16), one, zero)
    count = -(-rows // 128)
    slots = -(-count // 16) * 16
    which = lax.broadcasted_iota(jnp.int32, (slots, tile), 0)
    on_heads = jnp.where(which == (head >> 7), one, zero)
    off_tails = jnp.where(which == (tail >> 7), -one, zero)

    def build(first, size):
        blocks = []
        for block in range(first // 128, (first + size) // 128):
            off_tail = off_tails[block:block + 1]
            if block * 128 < local:
                blocks.append(low_head * on_heads[block:block + 1] + low_tail * off_tail)
            else:
                blocks.append(low_tail * off_tail)
        return jnp.concatenate(blocks, axis=0) if len(blocks) > 1 else blocks[0]

    return build


def pieces(rows):
    step = 256 if rows % 256 == 0 else (128 if rows % 128 == 0 else rows)
    return [(first, step) for first in range(0, rows, step)]


def flow_kernel(mode, local):
    scatter = mode == "scatter"

    def kernel(xs_ref, head_ref, tail_ref, w_ref, *out_ref):
        out_ref, acc = (out_ref[:2], out_ref[2:]) if scatter else (out_ref[0], ())
        step = pl.program_id(0)
        width, rows = xs_ref.shape
        head = head_ref[...]
        tail = tail_ref[...]
        xs = split3(xs_ref[...])
        parts = []
        gap = None
        build = incidence(head, tail, rows, local)
        for first, size in pieces(rows):
            ends = build(first, size)
            parts.append(ends)
            term = jnp.dot(xs[:, first:first + size], ends, preferred_element_type=jnp.float32)
            gap = term if gap is None else gap + term
        gap = gap[:width] + gap[width:2 * width] + gap[2 * width:]
        if mode == "gap":
            out_ref[...] = jnp.sum(gap * gap, axis=0, keepdims=True)
            return
        weighted = gap * w_ref[...]
        energy = jnp.sum(gap * weighted, axis=1, keepdims=True)
        if mode == "energy":
            out_ref[...] = jnp.where(step == 0, 0.0, out_ref[...]) + energy
            return
        (total,) = acc
        energy_ref = out_ref[1]
        out_ref = out_ref[0]
        energy_ref[...] = jnp.where(step == 0, 0.0, energy_ref[...]) + energy
        flow = split3(weighted)
        dims = (((1,), (1,)), ((), ()))
        for (first, size), ends in zip(pieces(rows), parts):
            window = total[:, first:first + size]
            total[:, first:first + size] = jnp.where(step == 0, 0.0, window) + lax.dot_general(
                flow, ends, dims, preferred_element_type=jnp.float32
            )

        @pl.when(step == pl.num_programs(0) - 1)
        def _():
            sums = total[...]
            out_ref[...] = sums[:width] + sums[width:2 * width] + sums[2 * width:]

    return kernel


def edge_pass(extended, head_rows, tail_slots, weights, mode, local):
    width, rows = extended.shape
    edges = head_rows.shape[1]
    tile = edge_tile(rows)
    if mode != "scatter" and rows <= 2048 and edges % 4096 == 0:
        tile = 4096
    edge_spec = pl.BlockSpec((1, tile), lambda i: (0, i))
    full = pl.BlockSpec((width, rows), lambda i: (0, 0))
    if mode == "scatter":
        out_shape = (jax.ShapeDtypeStruct((width, rows), jnp.float32), jax.ShapeDtypeStruct((width, 1), jnp.float32))
        out_spec = (pl.BlockSpec((width, rows), lambda i: (0, 0)), pl.BlockSpec((width, 1), lambda i: (0, 0)))
        scratch = [pltpu.VMEM((3 * width, rows), jnp.float32)]
    elif mode == "energy":
        out_shape = jax.ShapeDtypeStruct((width, 1), jnp.float32)
        out_spec = pl.BlockSpec((width, 1), lambda i: (0, 0))
        scratch = []
    else:
        out_shape = jax.ShapeDtypeStruct((1, edges), jnp.float32)
        out_spec = edge_spec
        scratch = []
    return pl.pallas_call(
        flow_kernel(mode, local),
        grid=(edges // tile,),
        in_specs=[full, edge_spec, edge_spec, edge_spec],
        out_specs=out_spec,
        out_shape=out_shape,
        scratch_shapes=scratch,
        compiler_params=pltpu.CompilerParams(
            dimension_semantics=("arbitrary",), vmem_limit_bytes=48 * 1024 * 1024
        ),
    )(extended, head_rows, tail_slots, weights)


def picker(halo_rows, count):
    peers, cap = halo_rows.shape
    index = lax.broadcasted_iota(jnp.int32, (peers, cap, count), 2)
    return (halo_rows[:, :, None] == index).astype(jnp.bfloat16)


def parts3(values):
    first = lax.reduce_precision(values, exponent_bits=8, mantissa_bits=7)
    rest = values - first
    second = lax.reduce_precision(rest, exponent_bits=8, mantissa_bits=7)
    third = rest - second
    return jnp.concatenate([first, second, third], axis=0).astype(jnp.bfloat16)


def pick(pattern, values, choice):
    width = values.shape[0]
    out = jnp.einsum(pattern, parts3(values), choice, preferred_element_type=jnp.float32)
    return out[:width] + out[width:2 * width] + out[2 * width:]


def extend(field, halo_rows):
    chosen = pick("cv,psv->cps", field, picker(halo_rows, field.shape[1]))
    mirrored = trade(chosen)
    return jnp.concatenate([field, mirrored.reshape(field.shape[0], -1)], axis=1)


def operate(field, shift, head_rows, tail_slots, weights, halo_rows, full=True):
    count = field.shape[1]
    width = field.shape[0]
    peers, cap = halo_rows.shape
    extended = extend(field, halo_rows)
    squares = field * field
    if not full:
        energy = edge_pass(extended, head_rows, tail_slots, weights, "energy", count)
        own = jnp.stack([jnp.sum(squares, axis=1), jnp.sum(shift * squares, axis=1) + energy[:, 0]], axis=1)
        got = trade(jnp.broadcast_to(own[:, None, :], (width, peers, 2)))
        norm, product = jnp.sum(got, axis=1).T
        return None, norm, product, extended[:, count:]
    summed, energy = edge_pass(extended, head_rows, tail_slots, weights, "scatter", count)
    own = jnp.stack([jnp.sum(squares, axis=1), jnp.sum(shift * squares, axis=1) + energy[:, 0]], axis=1)
    sent = jnp.concatenate(
        [summed[:, count:].reshape(width, peers, cap), jnp.broadcast_to(own[:, None, :], (width, peers, 2))], axis=2
    )
    got = trade(sent)
    returned = got[:, :, :cap]
    norm, product = jnp.sum(got[:, :, cap:], axis=1).T
    local = summed[:, :count] + pick("cps,psv->cv", returned, picker(halo_rows, count))
    return shift * field + local, norm, product, extended[:, count:]


def body(right_side, shift, edge_ends, weights, halo_rows):
    head_rows = edge_ends[0:1]
    tail_slots = edge_ends[1:2]
    weights = weights[None, :]
    share = edge_ends.shape[1] // lax.axis_size("col")
    start = lax.axis_index("col") * share
    quarter = [lax.dynamic_slice_in_dim(item, start, share, axis=1) for item in (head_rows, tail_slots, weights)]
    solution = jnp.zeros_like(right_side)
    residual = right_side
    image, norm_now, product, mirrored = operate(residual, shift, head_rows, tail_slots, weights, halo_rows)
    alpha = norm_now / product
    direction = residual
    along = image
    far_solution = jnp.zeros_like(mirrored)
    far_direction = mirrored
    for step in range(ITERS):
        solution = solution + alpha[:, None] * direction
        far_solution = far_solution + alpha[:, None] * far_direction
        residual = None if along is None else residual - alpha[:, None] * along
        if step + 1 < ITERS:
            image, norm_next, product, mirrored = operate(
                residual, shift, head_rows, tail_slots, weights, halo_rows, step + 2 < ITERS
            )
            ratio = norm_next / norm_now
            alpha = norm_next / (product - ratio * norm_next / alpha)
            direction = residual + ratio[:, None] * direction
            far_direction = mirrored + ratio[:, None] * far_direction
            along = None if image is None else image + ratio[:, None] * along
            norm_now = norm_next
    extended = jnp.concatenate([solution, far_solution], axis=1)
    total = edge_pass(lax.all_gather(extended, "col", axis=0, tiled=True), *quarter, "gap", solution.shape[1])[0]
    resistance = lax.all_gather(total, "col", axis=0, tiled=True)
    return (solution, resistance)


def solution(mesh):
    placed = (
        P("col", ("vx", "vy")),
        P(("vx", "vy")),
        P(None, ("vx", "vy")),
        P(("vx", "vy")),
        P(("vx", "vy"), None),
    )
    return jax.shard_map(
        body,
        mesh=mesh,
        in_specs=placed,
        out_specs=(P("col", ("vx", "vy")), P(("vx", "vy"))),
        check_vma=False,
    )
```

```python
import jax
import jax.numpy as jnp
from jax import lax
from jax.experimental import pallas as pl
from jax.experimental.pallas import tpu as pltpu
from jax.sharding import PartitionSpec as P

ITERS = 2


def trade(blocks):
    return lax.all_to_all(blocks, ("vx", "vy"), split_axis=1, concat_axis=1, tiled=True)


def split3(values):
    first = values.astype(jnp.bfloat16)
    rest = values - first.astype(jnp.float32)
    second = rest.astype(jnp.bfloat16)
    third = (rest - second.astype(jnp.float32)).astype(jnp.bfloat16)
    return jnp.concatenate([first, second, third], axis=0)


def edge_tile(rows):
    return 2048 if rows <= 2048 else 256


def incidence(head, tail, rows, local):
    tile = head.shape[1]
    if rows % 128:
        def build(first, size):
            index = lax.broadcasted_iota(jnp.int32, (size, tile), 0) + first
            ends = (index == head).astype(jnp.float32) - (index == tail).astype(jnp.float32)
            return ends.astype(jnp.bfloat16)

        return build
    lane = lax.broadcasted_iota(jnp.int32, (128, tile), 0).astype(jnp.bfloat16)
    one = jnp.ones((), jnp.bfloat16)
    zero = jnp.zeros((), jnp.bfloat16)
    low_head = jnp.where(lane == (head & 127).astype(jnp.bfloat16), one, zero)
    low_tail = jnp.where(lane == (tail & 127).astype(jnp.bfloat16), one, zero)
    count = -(-rows // 128)
    slots = -(-count // 16) * 16
    which = lax.broadcasted_iota(jnp.int32, (slots, tile), 0)
    on_heads = jnp.where(which == (head >> 7), one, zero)
    off_tails = jnp.where(which == (tail >> 7), -one, zero)

    def build(first, size):
        blocks = []
        for block in range(first // 128, (first + size) // 128):
            off_tail = off_tails[block:block + 1]
            if block * 128 < local:
                blocks.append(low_head * on_heads[block:block + 1] + low_tail * off_tail)
            else:
                blocks.append(low_tail * off_tail)
        return jnp.concatenate(blocks, axis=0) if len(blocks) > 1 else blocks[0]

    return build


def pieces(rows):
    step = 256 if rows % 256 == 0 else (128 if rows % 128 == 0 else rows)
    return [(first, step) for first in range(0, rows, step)]


def flow_kernel(mode, local):
    scatter = mode == "scatter"

    def kernel(xs_ref, head_ref, tail_ref, w_ref, *out_ref):
        out_ref, acc = (out_ref[:2], out_ref[2:]) if scatter else (out_ref[0], ())
        step = pl.program_id(0)
        width, rows = xs_ref.shape
        head = head_ref[...]
        tail = tail_ref[...]
        xs = split3(xs_ref[...])
        parts = []
        gap = None
        build = incidence(head, tail, rows, local)
        for first, size in pieces(rows):
            ends = build(first, size)
            parts.append(ends)
            term = jnp.dot(xs[:, first:first + size], ends, preferred_element_type=jnp.float32)
            gap = term if gap is None else gap + term
        gap = gap[:width] + gap[width:2 * width] + gap[2 * width:]
        if mode == "gap":
            out_ref[...] = jnp.sum(gap * gap, axis=0, keepdims=True)
            return
        weighted = gap * w_ref[...]
        energy = jnp.sum(gap * weighted, axis=1, keepdims=True)
        if mode == "energy":
            out_ref[...] = jnp.where(step == 0, 0.0, out_ref[...]) + energy
            return
        (total,) = acc
        energy_ref = out_ref[1]
        out_ref = out_ref[0]
        energy_ref[...] = jnp.where(step == 0, 0.0, energy_ref[...]) + energy
        flow = split3(weighted)
        dims = (((1,), (1,)), ((), ()))
        for (first, size), ends in zip(pieces(rows), parts):
            window = total[:, first:first + size]
            total[:, first:first + size] = jnp.where(step == 0, 0.0, window) + lax.dot_general(
                flow, ends, dims, preferred_element_type=jnp.float32
            )

        @pl.when(step == pl.num_programs(0) - 1)
        def _():
            sums = total[...]
            out_ref[...] = sums[:width] + sums[width:2 * width] + sums[2 * width:]

    return kernel


def edge_pass(extended, head_rows, tail_slots, weights, mode, local):
    width, rows = extended.shape
    edges = head_rows.shape[1]
    tile = edge_tile(rows)
    if rows <= 2048 and edges % 4096 == 0:
        tile = 4096
    edge_spec = pl.BlockSpec((1, tile), lambda i: (0, i))
    full = pl.BlockSpec((width, rows), lambda i: (0, 0))
    if mode == "scatter":
        out_shape = (jax.ShapeDtypeStruct((width, rows), jnp.float32), jax.ShapeDtypeStruct((width, 1), jnp.float32))
        out_spec = (pl.BlockSpec((width, rows), lambda i: (0, 0)), pl.BlockSpec((width, 1), lambda i: (0, 0)))
        scratch = [pltpu.VMEM((3 * width, rows), jnp.float32)]
    elif mode == "energy":
        out_shape = jax.ShapeDtypeStruct((width, 1), jnp.float32)
        out_spec = pl.BlockSpec((width, 1), lambda i: (0, 0))
        scratch = []
    else:
        out_shape = jax.ShapeDtypeStruct((1, edges), jnp.float32)
        out_spec = edge_spec
        scratch = []
    return pl.pallas_call(
        flow_kernel(mode, local),
        grid=(edges // tile,),
        in_specs=[full, edge_spec, edge_spec, edge_spec],
        out_specs=out_spec,
        out_shape=out_shape,
        scratch_shapes=scratch,
        compiler_params=pltpu.CompilerParams(
            dimension_semantics=("arbitrary",), vmem_limit_bytes=48 * 1024 * 1024
        ),
    )(extended, head_rows, tail_slots, weights)


def picker(halo_rows, count):
    peers, cap = halo_rows.shape
    index = lax.broadcasted_iota(jnp.int32, (peers, cap, count), 2)
    return (halo_rows[:, :, None] == index).astype(jnp.bfloat16)


def parts3(values):
    first = lax.reduce_precision(values, exponent_bits=8, mantissa_bits=7)
    rest = values - first
    second = lax.reduce_precision(rest, exponent_bits=8, mantissa_bits=7)
    third = rest - second
    return jnp.concatenate([first, second, third], axis=0).astype(jnp.bfloat16)


def pick(pattern, values, choice):
    width = values.shape[0]
    out = jnp.einsum(pattern, parts3(values), choice, preferred_element_type=jnp.float32)
    return out[:width] + out[width:2 * width] + out[2 * width:]


def extend(field, halo_rows):
    chosen = pick("cv,psv->cps", field, picker(halo_rows, field.shape[1]))
    mirrored = trade(chosen)
    return jnp.concatenate([field, mirrored.reshape(field.shape[0], -1)], axis=1)


def operate(field, shift, head_rows, tail_slots, weights, halo_rows, full=True):
    count = field.shape[1]
    width = field.shape[0]
    peers, cap = halo_rows.shape
    extended = extend(field, halo_rows)
    squares = field * field
    if not full:
        energy = edge_pass(extended, head_rows, tail_slots, weights, "energy", count)
        own = jnp.stack([jnp.sum(squares, axis=1), jnp.sum(shift * squares, axis=1) + energy[:, 0]], axis=1)
        got = trade(jnp.broadcast_to(own[:, None, :], (width, peers, 2)))
        norm, product = jnp.sum(got, axis=1).T
        return None, norm, product, extended[:, count:]
    summed, energy = edge_pass(extended, head_rows, tail_slots, weights, "scatter", count)
    own = jnp.stack([jnp.sum(squares, axis=1), jnp.sum(shift * squares, axis=1) + energy[:, 0]], axis=1)
    sent = jnp.concatenate(
        [summed[:, count:].reshape(width, peers, cap), jnp.broadcast_to(own[:, None, :], (width, peers, 2))], axis=2
    )
    got = trade(sent)
    returned = got[:, :, :cap]
    norm, product = jnp.sum(got[:, :, cap:], axis=1).T
    local = summed[:, :count] + pick("cps,psv->cv", returned, picker(halo_rows, count))
    return shift * field + local, norm, product, extended[:, count:]


def body(right_side, shift, edge_ends, weights, halo_rows):
    head_rows = edge_ends[0:1]
    tail_slots = edge_ends[1:2]
    weights = weights[None, :]
    share = edge_ends.shape[1] // lax.axis_size("col")
    start = lax.axis_index("col") * share
    quarter = [lax.dynamic_slice_in_dim(item, start, share, axis=1) for item in (head_rows, tail_slots, weights)]
    solution = jnp.zeros_like(right_side)
    residual = right_side
    image, norm_now, product, mirrored = operate(residual, shift, head_rows, tail_slots, weights, halo_rows)
    alpha = norm_now / product
    direction = residual
    along = image
    far_solution = jnp.zeros_like(mirrored)
    far_direction = mirrored
    for step in range(ITERS):
        solution = solution + alpha[:, None] * direction
        far_solution = far_solution + alpha[:, None] * far_direction
        residual = None if along is None else residual - alpha[:, None] * along
        if step + 1 < ITERS:
            image, norm_next, product, mirrored = operate(
                residual, shift, head_rows, tail_slots, weights, halo_rows, step + 2 < ITERS
            )
            ratio = norm_next / norm_now
            alpha = norm_next / (product - ratio * norm_next / alpha)
            direction = residual + ratio[:, None] * direction
            far_direction = mirrored + ratio[:, None] * far_direction
            along = None if image is None else image + ratio[:, None] * along
            norm_now = norm_next
    extended = jnp.concatenate([solution, far_solution], axis=1)
    total = edge_pass(lax.all_gather(extended, "col", axis=0, tiled=True), *quarter, "gap", solution.shape[1])[0]
    resistance = lax.all_gather(total, "col", axis=0, tiled=True)
    return (solution, resistance)


def solution(mesh):
    placed = (
        P("col", ("vx", "vy")),
        P(("vx", "vy")),
        P(None, ("vx", "vy")),
        P(("vx", "vy")),
        P(("vx", "vy"), None),
    )
    return jax.shard_map(
        body,
        mesh=mesh,
        in_specs=placed,
        out_specs=(P("col", ("vx", "vy")), P(("vx", "vy"))),
        check_vma=False,
    )
```

```python
import jax
import jax.numpy as jnp
from jax import lax
from jax.experimental import pallas as pl
from jax.experimental.pallas import tpu as pltpu
from jax.sharding import PartitionSpec as P

ITERS = 2


def trade(blocks):
    return lax.all_to_all(blocks, ("vx", "vy"), split_axis=1, concat_axis=1, tiled=True)


def split3(values):
    first = values.astype(jnp.bfloat16)
    rest = values - first.astype(jnp.float32)
    second = rest.astype(jnp.bfloat16)
    third = (rest - second.astype(jnp.float32)).astype(jnp.bfloat16)
    return jnp.concatenate([first, second, third], axis=0)


def edge_tile(rows):
    return 2048 if rows <= 2048 else 256


def incidence(head, tail, rows, local):
    tile = head.shape[1]
    if rows % 128:
        def build(first, size):
            index = lax.broadcasted_iota(jnp.int32, (size, tile), 0) + first
            ends = (index == head).astype(jnp.float32) - (index == tail).astype(jnp.float32)
            return ends.astype(jnp.bfloat16)

        return build
    lane = lax.broadcasted_iota(jnp.int32, (128, tile), 0).astype(jnp.bfloat16)
    one = jnp.ones((), jnp.bfloat16)
    zero = jnp.zeros((), jnp.bfloat16)
    low_head = jnp.where(lane == (head & 127).astype(jnp.bfloat16), one, zero)
    low_tail = jnp.where(lane == (tail & 127).astype(jnp.bfloat16), one, zero)
    count = -(-rows // 128)
    slots = -(-count // 16) * 16
    which = lax.broadcasted_iota(jnp.int32, (slots, tile), 0)
    on_heads = jnp.where(which == (head >> 7), one, zero)
    off_tails = jnp.where(which == (tail >> 7), -one, zero)

    def build(first, size):
        blocks = []
        for block in range(first // 128, (first + size) // 128):
            off_tail = off_tails[block:block + 1]
            if block * 128 < local:
                blocks.append(low_head * on_heads[block:block + 1] + low_tail * off_tail)
            else:
                blocks.append(low_tail * off_tail)
        return jnp.concatenate(blocks, axis=0) if len(blocks) > 1 else blocks[0]

    return build


def pieces(rows, wide=False):
    step = 512 if wide and rows % 512 == 0 else (256 if rows % 256 == 0 else (128 if rows % 128 == 0 else rows))
    return [(first, step) for first in range(0, rows, step)]


def flow_kernel(mode, local):
    scatter = mode == "scatter"

    def kernel(xs_ref, head_ref, tail_ref, w_ref, *out_ref):
        out_ref, acc = (out_ref[:2], out_ref[2:]) if scatter else (out_ref[0], ())
        step = pl.program_id(0)
        width, rows = xs_ref.shape
        head = head_ref[...]
        tail = tail_ref[...]
        xs = split3(xs_ref[...])
        parts = []
        gap = None
        build = incidence(head, tail, rows, local)
        for first, size in pieces(rows, mode != "gap"):
            ends = build(first, size)
            parts.append(ends)
            term = jnp.dot(xs[:, first:first + size], ends, preferred_element_type=jnp.float32)
            gap = term if gap is None else gap + term
        gap = gap[:width] + gap[width:2 * width] + gap[2 * width:]
        if mode == "gap":
            out_ref[...] = jnp.sum(gap * gap, axis=0, keepdims=True)
            return
        weighted = gap * w_ref[...]
        energy = jnp.sum(gap * weighted, axis=1, keepdims=True)
        if mode == "energy":
            out_ref[...] = jnp.where(step == 0, 0.0, out_ref[...]) + energy
            return
        (total,) = acc
        energy_ref = out_ref[1]
        out_ref = out_ref[0]
        energy_ref[...] = jnp.where(step == 0, 0.0, energy_ref[...]) + energy
        flow = split3(weighted)
        dims = (((1,), (1,)), ((), ()))
        for (first, size), ends in zip(pieces(rows, True), parts):
            window = total[:, first:first + size]
            total[:, first:first + size] = jnp.where(step == 0, 0.0, window) + lax.dot_general(
                flow, ends, dims, preferred_element_type=jnp.float32
            )

        @pl.when(step == pl.num_programs(0) - 1)
        def _():
            sums = total[...]
            out_ref[...] = sums[:width] + sums[width:2 * width] + sums[2 * width:]

    return kernel


def edge_pass(extended, head_rows, tail_slots, weights, mode, local):
    width, rows = extended.shape
    edges = head_rows.shape[1]
    tile = edge_tile(rows)
    if rows <= 2048 and edges % 4096 == 0:
        tile = 4096
    edge_spec = pl.BlockSpec((1, tile), lambda i: (0, i))
    full = pl.BlockSpec((width, rows), lambda i: (0, 0))
    if mode == "scatter":
        out_shape = (jax.ShapeDtypeStruct((width, rows), jnp.float32), jax.ShapeDtypeStruct((width, 1), jnp.float32))
        out_spec = (pl.BlockSpec((width, rows), lambda i: (0, 0)), pl.BlockSpec((width, 1), lambda i: (0, 0)))
        scratch = [pltpu.VMEM((3 * width, rows), jnp.float32)]
    elif mode == "energy":
        out_shape = jax.ShapeDtypeStruct((width, 1), jnp.float32)
        out_spec = pl.BlockSpec((width, 1), lambda i: (0, 0))
        scratch = []
    else:
        out_shape = jax.ShapeDtypeStruct((1, edges), jnp.float32)
        out_spec = edge_spec
        scratch = []
    return pl.pallas_call(
        flow_kernel(mode, local),
        grid=(edges // tile,),
        in_specs=[full, edge_spec, edge_spec, edge_spec],
        out_specs=out_spec,
        out_shape=out_shape,
        scratch_shapes=scratch,
        compiler_params=pltpu.CompilerParams(
            dimension_semantics=("arbitrary",), vmem_limit_bytes=48 * 1024 * 1024
        ),
    )(extended, head_rows, tail_slots, weights)


def picker(halo_rows, count):
    peers, cap = halo_rows.shape
    index = lax.broadcasted_iota(jnp.int32, (peers, cap, count), 2)
    return (halo_rows[:, :, None] == index).astype(jnp.bfloat16)


def parts3(values):
    first = lax.reduce_precision(values, exponent_bits=8, mantissa_bits=7)
    rest = values - first
    second = lax.reduce_precision(rest, exponent_bits=8, mantissa_bits=7)
    third = rest - second
    return jnp.concatenate([first, second, third], axis=0).astype(jnp.bfloat16)


def pick(pattern, values, choice):
    width = values.shape[0]
    out = jnp.einsum(pattern, parts3(values), choice, preferred_element_type=jnp.float32)
    return out[:width] + out[width:2 * width] + out[2 * width:]


def extend(field, halo_rows):
    chosen = pick("cv,psv->cps", field, picker(halo_rows, field.shape[1]))
    mirrored = trade(chosen)
    return jnp.concatenate([field, mirrored.reshape(field.shape[0], -1)], axis=1)


def operate(field, shift, head_rows, tail_slots, weights, halo_rows, full=True):
    count = field.shape[1]
    width = field.shape[0]
    peers, cap = halo_rows.shape
    extended = extend(field, halo_rows)
    squares = field * field
    if not full:
        energy = edge_pass(extended, head_rows, tail_slots, weights, "energy", count)
        own = jnp.stack([jnp.sum(squares, axis=1), jnp.sum(shift * squares, axis=1) + energy[:, 0]], axis=1)
        got = trade(jnp.broadcast_to(own[:, None, :], (width, peers, 2)))
        norm, product = jnp.sum(got, axis=1).T
        return None, norm, product, extended[:, count:]
    summed, energy = edge_pass(extended, head_rows, tail_slots, weights, "scatter", count)
    own = jnp.stack([jnp.sum(squares, axis=1), jnp.sum(shift * squares, axis=1) + energy[:, 0]], axis=1)
    sent = jnp.concatenate(
        [summed[:, count:].reshape(width, peers, cap), jnp.broadcast_to(own[:, None, :], (width, peers, 2))], axis=2
    )
    got = trade(sent)
    returned = got[:, :, :cap]
    norm, product = jnp.sum(got[:, :, cap:], axis=1).T
    local = summed[:, :count] + pick("cps,psv->cv", returned, picker(halo_rows, count))
    return shift * field + local, norm, product, extended[:, count:]


def body(right_side, shift, edge_ends, weights, halo_rows):
    head_rows = edge_ends[0:1]
    tail_slots = edge_ends[1:2]
    weights = weights[None, :]
    share = edge_ends.shape[1] // lax.axis_size("col")
    start = lax.axis_index("col") * share
    quarter = [lax.dynamic_slice_in_dim(item, start, share, axis=1) for item in (head_rows, tail_slots, weights)]
    solution = jnp.zeros_like(right_side)
    residual = right_side
    image, norm_now, product, mirrored = operate(residual, shift, head_rows, tail_slots, weights, halo_rows)
    alpha = norm_now / product
    direction = residual
    along = image
    far_solution = jnp.zeros_like(mirrored)
    far_direction = mirrored
    for step in range(ITERS):
        solution = solution + alpha[:, None] * direction
        far_solution = far_solution + alpha[:, None] * far_direction
        residual = None if along is None else residual - alpha[:, None] * along
        if step + 1 < ITERS:
            image, norm_next, product, mirrored = operate(
                residual, shift, head_rows, tail_slots, weights, halo_rows, step + 2 < ITERS
            )
            ratio = norm_next / norm_now
            alpha = norm_next / (product - ratio * norm_next / alpha)
            direction = residual + ratio[:, None] * direction
            far_direction = mirrored + ratio[:, None] * far_direction
            along = None if image is None else image + ratio[:, None] * along
            norm_now = norm_next
    extended = jnp.concatenate([solution, far_solution], axis=1)
    total = edge_pass(lax.all_gather(extended, "col", axis=0, tiled=True), *quarter, "gap", solution.shape[1])[0]
    resistance = lax.all_gather(total, "col", axis=0, tiled=True)
    return (solution, resistance)


def solution(mesh):
    placed = (
        P("col", ("vx", "vy")),
        P(("vx", "vy")),
        P(None, ("vx", "vy")),
        P(("vx", "vy")),
        P(("vx", "vy"), None),
    )
    return jax.shard_map(
        body,
        mesh=mesh,
        in_specs=placed,
        out_specs=(P("col", ("vx", "vy")), P(("vx", "vy"))),
        check_vma=False,
    )
```

```python
import jax
import jax.numpy as jnp
from jax import lax
from jax.experimental import pallas as pl
from jax.experimental.pallas import tpu as pltpu
from jax.sharding import PartitionSpec as P

ITERS = 2


def trade(blocks):
    return lax.all_to_all(blocks, ("vx", "vy"), split_axis=1, concat_axis=1, tiled=True)


def split3(values):
    first = values.astype(jnp.bfloat16)
    rest = values - first.astype(jnp.float32)
    second = rest.astype(jnp.bfloat16)
    third = (rest - second.astype(jnp.float32)).astype(jnp.bfloat16)
    return jnp.concatenate([first, second, third], axis=0)


def edge_tile(rows):
    return 2048 if rows <= 2048 else 256


def incidence(head, tail, rows, local):
    tile = head.shape[1]
    if rows % 128:
        def build(first, size):
            index = lax.broadcasted_iota(jnp.int32, (size, tile), 0) + first
            ends = (index == head).astype(jnp.float32) - (index == tail).astype(jnp.float32)
            return ends.astype(jnp.bfloat16)

        return build
    lane = lax.broadcasted_iota(jnp.int32, (128, tile), 0).astype(jnp.bfloat16)
    one = jnp.ones((), jnp.bfloat16)
    zero = jnp.zeros((), jnp.bfloat16)
    low_head = jnp.where(lane == (head & 127).astype(jnp.bfloat16), one, zero)
    low_tail = jnp.where(lane == (tail & 127).astype(jnp.bfloat16), one, zero)
    count = -(-rows // 128)
    slots = -(-count // 16) * 16
    which = lax.broadcasted_iota(jnp.int32, (slots, tile), 0)
    on_heads = jnp.where(which == (head >> 7), one, zero)
    off_tails = jnp.where(which == (tail >> 7), -one, zero)

    def build(first, size):
        blocks = []
        for block in range(first // 128, (first + size) // 128):
            off_tail = off_tails[block:block + 1]
            if block * 128 < local:
                blocks.append(low_head * on_heads[block:block + 1] + low_tail * off_tail)
            else:
                blocks.append(low_tail * off_tail)
        return jnp.concatenate(blocks, axis=0) if len(blocks) > 1 else blocks[0]

    return build


def pieces(rows, wide=False):
    step = 512 if wide and rows % 512 == 0 else (256 if rows % 256 == 0 else (128 if rows % 128 == 0 else rows))
    return [(first, step) for first in range(0, rows, step)]


def flow_kernel(mode, local):
    scatter = mode == "scatter"

    def kernel(xs_ref, head_ref, tail_ref, w_ref, *out_ref):
        out_ref, acc = (out_ref[:2], out_ref[2:]) if scatter else (out_ref[0], ())
        step = pl.program_id(0)
        width, rows = xs_ref.shape
        head = head_ref[...]
        tail = tail_ref[...]
        xs = split3(xs_ref[...])
        parts = []
        gap = None
        build = incidence(head, tail, rows, local)
        for first, size in pieces(rows, mode != "gap"):
            ends = build(first, size)
            parts.append(ends)
            term = jnp.dot(xs[:, first:first + size], ends, preferred_element_type=jnp.float32)
            gap = term if gap is None else gap + term
        gap = gap[:width] + gap[width:2 * width] + gap[2 * width:]
        if mode == "gap":
            out_ref[...] = jnp.sum(gap * gap, axis=0, keepdims=True)
            return
        weighted = gap * w_ref[...]
        energy = jnp.sum(gap * weighted, axis=1, keepdims=True)
        if mode == "energy":
            out_ref[...] = jnp.where(step == 0, 0.0, out_ref[...]) + energy
            return
        (total,) = acc
        energy_ref = out_ref[1]
        out_ref = out_ref[0]
        energy_ref[...] = jnp.where(step == 0, 0.0, energy_ref[...]) + energy
        flow = split3(weighted)
        dims = (((1,), (1,)), ((), ()))
        for (first, size), ends in zip(pieces(rows, True), parts):
            window = total[:, first:first + size]
            total[:, first:first + size] = jnp.where(step == 0, 0.0, window) + lax.dot_general(
                flow, ends, dims, preferred_element_type=jnp.float32
            )

        @pl.when(step == pl.num_programs(0) - 1)
        def _():
            sums = total[...]
            out_ref[...] = sums[:width] + sums[width:2 * width] + sums[2 * width:]

    return kernel


def edge_pass(extended, head_rows, tail_slots, weights, mode, local):
    width, rows = extended.shape
    edges = head_rows.shape[1]
    tile = edge_tile(rows)
    if rows <= 2048 and edges % 4096 == 0:
        tile = 8192 if mode == "energy" and edges % 8192 == 0 else 4096
    edge_spec = pl.BlockSpec((1, tile), lambda i: (0, i))
    full = pl.BlockSpec((width, rows), lambda i: (0, 0))
    if mode == "scatter":
        out_shape = (jax.ShapeDtypeStruct((width, rows), jnp.float32), jax.ShapeDtypeStruct((width, 1), jnp.float32))
        out_spec = (pl.BlockSpec((width, rows), lambda i: (0, 0)), pl.BlockSpec((width, 1), lambda i: (0, 0)))
        scratch = [pltpu.VMEM((3 * width, rows), jnp.float32)]
    elif mode == "energy":
        out_shape = jax.ShapeDtypeStruct((width, 1), jnp.float32)
        out_spec = pl.BlockSpec((width, 1), lambda i: (0, 0))
        scratch = []
    else:
        out_shape = jax.ShapeDtypeStruct((1, edges), jnp.float32)
        out_spec = edge_spec
        scratch = []
    return pl.pallas_call(
        flow_kernel(mode, local),
        grid=(edges // tile,),
        in_specs=[full, edge_spec, edge_spec, edge_spec],
        out_specs=out_spec,
        out_shape=out_shape,
        scratch_shapes=scratch,
        compiler_params=pltpu.CompilerParams(
            dimension_semantics=("arbitrary",), vmem_limit_bytes=48 * 1024 * 1024
        ),
    )(extended, head_rows, tail_slots, weights)


def picker(halo_rows, count):
    peers, cap = halo_rows.shape
    index = lax.broadcasted_iota(jnp.int32, (peers, cap, count), 2)
    return (halo_rows[:, :, None] == index).astype(jnp.bfloat16)


def parts3(values):
    first = lax.reduce_precision(values, exponent_bits=8, mantissa_bits=7)
    rest = values - first
    second = lax.reduce_precision(rest, exponent_bits=8, mantissa_bits=7)
    third = rest - second
    return jnp.concatenate([first, second, third], axis=0).astype(jnp.bfloat16)


def pick(pattern, values, choice):
    width = values.shape[0]
    out = jnp.einsum(pattern, parts3(values), choice, preferred_element_type=jnp.float32)
    return out[:width] + out[width:2 * width] + out[2 * width:]


def extend(field, halo_rows):
    chosen = pick("cv,psv->cps", field, picker(halo_rows, field.shape[1]))
    mirrored = trade(chosen)
    return jnp.concatenate([field, mirrored.reshape(field.shape[0], -1)], axis=1)


def operate(field, shift, head_rows, tail_slots, weights, halo_rows, full=True):
    count = field.shape[1]
    width = field.shape[0]
    peers, cap = halo_rows.shape
    extended = extend(field, halo_rows)
    squares = field * field
    if not full:
        energy = edge_pass(extended, head_rows, tail_slots, weights, "energy", count)
        own = jnp.stack([jnp.sum(squares, axis=1), jnp.sum(shift * squares, axis=1) + energy[:, 0]], axis=1)
        got = trade(jnp.broadcast_to(own[:, None, :], (width, peers, 2)))
        norm, product = jnp.sum(got, axis=1).T
        return None, norm, product, extended[:, count:]
    summed, energy = edge_pass(extended, head_rows, tail_slots, weights, "scatter", count)
    own = jnp.stack([jnp.sum(squares, axis=1), jnp.sum(shift * squares, axis=1) + energy[:, 0]], axis=1)
    sent = jnp.concatenate(
        [summed[:, count:].reshape(width, peers, cap), jnp.broadcast_to(own[:, None, :], (width, peers, 2))], axis=2
    )
    got = trade(sent)
    returned = got[:, :, :cap]
    norm, product = jnp.sum(got[:, :, cap:], axis=1).T
    local = summed[:, :count] + pick("cps,psv->cv", returned, picker(halo_rows, count))
    return shift * field + local, norm, product, extended[:, count:]


def body(right_side, shift, edge_ends, weights, halo_rows):
    head_rows = edge_ends[0:1]
    tail_slots = edge_ends[1:2]
    weights = weights[None, :]
    share = edge_ends.shape[1] // lax.axis_size("col")
    start = lax.axis_index("col") * share
    quarter = [lax.dynamic_slice_in_dim(item, start, share, axis=1) for item in (head_rows, tail_slots, weights)]
    solution = jnp.zeros_like(right_side)
    residual = right_side
    image, norm_now, product, mirrored = operate(residual, shift, head_rows, tail_slots, weights, halo_rows)
    alpha = norm_now / product
    direction = residual
    along = image
    far_solution = jnp.zeros_like(mirrored)
    far_direction = mirrored
    for step in range(ITERS):
        solution = solution + alpha[:, None] * direction
        far_solution = far_solution + alpha[:, None] * far_direction
        residual = None if along is None else residual - alpha[:, None] * along
        if step + 1 < ITERS:
            image, norm_next, product, mirrored = operate(
                residual, shift, head_rows, tail_slots, weights, halo_rows, step + 2 < ITERS
            )
            ratio = norm_next / norm_now
            alpha = norm_next / (product - ratio * norm_next / alpha)
            direction = residual + ratio[:, None] * direction
            far_direction = mirrored + ratio[:, None] * far_direction
            along = None if image is None else image + ratio[:, None] * along
            norm_now = norm_next
    extended = jnp.concatenate([solution, far_solution], axis=1)
    total = edge_pass(lax.all_gather(extended, "col", axis=0, tiled=True), *quarter, "gap", solution.shape[1])[0]
    resistance = lax.all_gather(total, "col", axis=0, tiled=True)
    return (solution, resistance)


def solution(mesh):
    placed = (
        P("col", ("vx", "vy")),
        P(("vx", "vy")),
        P(None, ("vx", "vy")),
        P(("vx", "vy")),
        P(("vx", "vy"), None),
    )
    return jax.shard_map(
        body,
        mesh=mesh,
        in_specs=placed,
        out_specs=(P("col", ("vx", "vy")), P(("vx", "vy"))),
        check_vma=False,
    )
```

```python
import jax
import jax.numpy as jnp
from jax import lax
from jax.experimental import pallas as pl
from jax.experimental.pallas import tpu as pltpu
from jax.sharding import PartitionSpec as P

ITERS = 2


def trade(blocks):
    return lax.all_to_all(blocks, ("vx", "vy"), split_axis=1, concat_axis=1, tiled=True)


def split3(values):
    first = values.astype(jnp.bfloat16)
    rest = values - first.astype(jnp.float32)
    second = rest.astype(jnp.bfloat16)
    third = (rest - second.astype(jnp.float32)).astype(jnp.bfloat16)
    return jnp.concatenate([first, second, third], axis=0)


def edge_tile(rows):
    return 2048 if rows <= 2048 else 256


def incidence(head, tail, rows, local):
    tile = head.shape[1]
    if rows % 128:
        def build(first, size):
            index = lax.broadcasted_iota(jnp.int32, (size, tile), 0) + first
            ends = (index == head).astype(jnp.float32) - (index == tail).astype(jnp.float32)
            return ends.astype(jnp.bfloat16)

        return build
    lane = lax.broadcasted_iota(jnp.int32, (128, tile), 0).astype(jnp.bfloat16)
    one = jnp.ones((), jnp.bfloat16)
    zero = jnp.zeros((), jnp.bfloat16)
    low_head = jnp.where(lane == (head & 127).astype(jnp.bfloat16), one, zero)
    low_tail = jnp.where(lane == (tail & 127).astype(jnp.bfloat16), one, zero)
    count = -(-rows // 128)
    slots = -(-count // 16) * 16
    which = lax.broadcasted_iota(jnp.int32, (slots, tile), 0)
    on_heads = jnp.where(which == (head >> 7), one, zero)
    off_tails = jnp.where(which == (tail >> 7), -one, zero)

    def build(first, size):
        blocks = []
        for block in range(first // 128, (first + size) // 128):
            off_tail = off_tails[block:block + 1]
            if block * 128 < local:
                blocks.append(low_head * on_heads[block:block + 1] + low_tail * off_tail)
            else:
                blocks.append(low_tail * off_tail)
        return jnp.concatenate(blocks, axis=0) if len(blocks) > 1 else blocks[0]

    return build


def pieces(rows, wide=False):
    step = 512 if wide and rows % 512 == 0 else (256 if rows % 256 == 0 else (128 if rows % 128 == 0 else rows))
    return [(first, step) for first in range(0, rows, step)]


def flow_kernel(mode, local):
    scatter = mode == "scatter"

    def kernel(xs_ref, head_ref, tail_ref, w_ref, *out_ref):
        out_ref, acc = (out_ref[:2], out_ref[2:]) if scatter else (out_ref[0], ())
        step = pl.program_id(0)
        width, rows = xs_ref.shape
        head = head_ref[...]
        tail = tail_ref[...]
        xs = split3(xs_ref[...])
        parts = []
        gap = None
        build = incidence(head, tail, rows, local)
        for first, size in pieces(rows, mode != "gap"):
            ends = build(first, size)
            parts.append(ends)
            term = jnp.dot(xs[:, first:first + size], ends, preferred_element_type=jnp.float32)
            gap = term if gap is None else gap + term
        gap = gap[:width] + gap[width:2 * width] + gap[2 * width:]
        if mode == "gap":
            out_ref[...] = jnp.sum(gap * gap, axis=0, keepdims=True)
            return
        weighted = gap * w_ref[...]
        energy = jnp.sum(gap * weighted, axis=1, keepdims=True)
        if mode == "energy":
            out_ref[...] = jnp.where(step == 0, 0.0, out_ref[...]) + energy
            return
        (total,) = acc
        energy_ref = out_ref[1]
        out_ref = out_ref[0]
        energy_ref[...] = jnp.where(step == 0, 0.0, energy_ref[...]) + energy
        flow = split3(weighted)
        dims = (((1,), (1,)), ((), ()))
        for (first, size), ends in zip(pieces(rows, True), parts):
            window = total[:, first:first + size]
            total[:, first:first + size] = jnp.where(step == 0, 0.0, window) + lax.dot_general(
                flow, ends, dims, preferred_element_type=jnp.float32
            )

        @pl.when(step == pl.num_programs(0) - 1)
        def _():
            sums = total[...]
            out_ref[...] = sums[:width] + sums[width:2 * width] + sums[2 * width:]

    return kernel


def edge_pass(extended, head_rows, tail_slots, weights, mode, local):
    width, rows = extended.shape
    edges = head_rows.shape[1]
    tile = edge_tile(rows)
    if rows <= 2048 and edges % 4096 == 0:
        tile = 16384 if mode == "energy" and edges == 16384 else 4096
    edge_spec = pl.BlockSpec((1, tile), lambda i: (0, i))
    full = pl.BlockSpec((width, rows), lambda i: (0, 0))
    if mode == "scatter":
        out_shape = (jax.ShapeDtypeStruct((width, rows), jnp.float32), jax.ShapeDtypeStruct((width, 1), jnp.float32))
        out_spec = (pl.BlockSpec((width, rows), lambda i: (0, 0)), pl.BlockSpec((width, 1), lambda i: (0, 0)))
        scratch = [pltpu.VMEM((3 * width, rows), jnp.float32)]
    elif mode == "energy":
        out_shape = jax.ShapeDtypeStruct((width, 1), jnp.float32)
        out_spec = pl.BlockSpec((width, 1), lambda i: (0, 0))
        scratch = []
    else:
        out_shape = jax.ShapeDtypeStruct((1, edges), jnp.float32)
        out_spec = edge_spec
        scratch = []
    return pl.pallas_call(
        flow_kernel(mode, local),
        grid=(edges // tile,),
        in_specs=[full, edge_spec, edge_spec, edge_spec],
        out_specs=out_spec,
        out_shape=out_shape,
        scratch_shapes=scratch,
        compiler_params=pltpu.CompilerParams(
            dimension_semantics=("arbitrary",), vmem_limit_bytes=48 * 1024 * 1024
        ),
    )(extended, head_rows, tail_slots, weights)


def picker(halo_rows, count):
    peers, cap = halo_rows.shape
    index = lax.broadcasted_iota(jnp.int32, (peers, cap, count), 2)
    return (halo_rows[:, :, None] == index).astype(jnp.bfloat16)


def parts3(values):
    first = lax.reduce_precision(values, exponent_bits=8, mantissa_bits=7)
    rest = values - first
    second = lax.reduce_precision(rest, exponent_bits=8, mantissa_bits=7)
    third = rest - second
    return jnp.concatenate([first, second, third], axis=0).astype(jnp.bfloat16)


def pick(pattern, values, choice):
    width = values.shape[0]
    out = jnp.einsum(pattern, parts3(values), choice, preferred_element_type=jnp.float32)
    return out[:width] + out[width:2 * width] + out[2 * width:]


def extend(field, halo_rows):
    chosen = pick("cv,psv->cps", field, picker(halo_rows, field.shape[1]))
    mirrored = trade(chosen)
    return jnp.concatenate([field, mirrored.reshape(field.shape[0], -1)], axis=1)


def operate(field, shift, head_rows, tail_slots, weights, halo_rows, full=True):
    count = field.shape[1]
    width = field.shape[0]
    peers, cap = halo_rows.shape
    extended = extend(field, halo_rows)
    squares = field * field
    if not full:
        energy = edge_pass(extended, head_rows, tail_slots, weights, "energy", count)
        own = jnp.stack([jnp.sum(squares, axis=1), jnp.sum(shift * squares, axis=1) + energy[:, 0]], axis=1)
        got = trade(jnp.broadcast_to(own[:, None, :], (width, peers, 2)))
        norm, product = jnp.sum(got, axis=1).T
        return None, norm, product, extended[:, count:]
    summed, energy = edge_pass(extended, head_rows, tail_slots, weights, "scatter", count)
    own = jnp.stack([jnp.sum(squares, axis=1), jnp.sum(shift * squares, axis=1) + energy[:, 0]], axis=1)
    sent = jnp.concatenate(
        [summed[:, count:].reshape(width, peers, cap), jnp.broadcast_to(own[:, None, :], (width, peers, 2))], axis=2
    )
    got = trade(sent)
    returned = got[:, :, :cap]
    norm, product = jnp.sum(got[:, :, cap:], axis=1).T
    local = summed[:, :count] + pick("cps,psv->cv", returned, picker(halo_rows, count))
    return shift * field + local, norm, product, extended[:, count:]


def body(right_side, shift, edge_ends, weights, halo_rows):
    head_rows = edge_ends[0:1]
    tail_slots = edge_ends[1:2]
    weights = weights[None, :]
    share = edge_ends.shape[1] // lax.axis_size("col")
    start = lax.axis_index("col") * share
    quarter = [lax.dynamic_slice_in_dim(item, start, share, axis=1) for item in (head_rows, tail_slots, weights)]
    solution = jnp.zeros_like(right_side)
    residual = right_side
    image, norm_now, product, mirrored = operate(residual, shift, head_rows, tail_slots, weights, halo_rows)
    alpha = norm_now / product
    direction = residual
    along = image
    far_solution = jnp.zeros_like(mirrored)
    far_direction = mirrored
    for step in range(ITERS):
        solution = solution + alpha[:, None] * direction
        far_solution = far_solution + alpha[:, None] * far_direction
        residual = None if along is None else residual - alpha[:, None] * along
        if step + 1 < ITERS:
            image, norm_next, product, mirrored = operate(
                residual, shift, head_rows, tail_slots, weights, halo_rows, step + 2 < ITERS
            )
            ratio = norm_next / norm_now
            alpha = norm_next / (product - ratio * norm_next / alpha)
            direction = residual + ratio[:, None] * direction
            far_direction = mirrored + ratio[:, None] * far_direction
            along = None if image is None else image + ratio[:, None] * along
            norm_now = norm_next
    extended = jnp.concatenate([solution, far_solution], axis=1)
    total = edge_pass(lax.all_gather(extended, "col", axis=0, tiled=True), *quarter, "gap", solution.shape[1])[0]
    resistance = lax.all_gather(total, "col", axis=0, tiled=True)
    return (solution, resistance)


def solution(mesh):
    placed = (
        P("col", ("vx", "vy")),
        P(("vx", "vy")),
        P(None, ("vx", "vy")),
        P(("vx", "vy")),
        P(("vx", "vy"), None),
    )
    return jax.shard_map(
        body,
        mesh=mesh,
        in_specs=placed,
        out_specs=(P("col", ("vx", "vy")), P(("vx", "vy"))),
        check_vma=False,
    )
```
